32 devices in a mesh: expert: 8 (over z, x), rep: 4 (over y, core).
Axes of the slice: x: 2, y: 2, z: 4, core: 2. Of those that a mesh axis runs over, the one named last changes fastest.
Arguments:
- tokens: bfloat16 [4, 2048, 2, 2048], P('rep', 'expert'), may hold values from -6 to 6
- expert_ids: int32 [4, 2048, 2, 2], P('rep', 'expert'), may hold values from 0 to 15, all different within a row; in each aligned block of 512 rows (0 to 511, 512 to 1023, ..., all dimensions but the last counted through in order) at most 80 rows name the same one
- gate_probs: float32 [4, 2048, 2, 2], P('rep', 'expert'), may hold values from 0.1 to 1
- norm_gain: float32 [2048], replicated, may hold values from 0.25 to 1.75
- expert_gate: bfloat16 [16, 2048, 1408], P('expert', None, 'rep'), may hold values from -0.125 to 0.125
- expert_up: bfloat16 [16, 2048, 1408], P('expert', None, 'rep'), may hold values from -0.125 to 0.125
- expert_down: bfloat16 [16, 1408, 2048], P('expert', 'rep'), may hold values from -0.15625 to 0.15625
- teacher_gain: float32 [2048], replicated, may hold values from 0.25 to 1.75
- teacher_qkv: bfloat16 [2048, 3, 16, 128], P(None, None, 'rep')
- qk_gain: float32 [2, 16, 128], P(None, 'rep'), may hold values from 0.5 to 7.5
- teacher_out: bfloat16 [16, 128, 2048], P('rep'), may hold values from -0.125 to 0.125
- critic_in: bfloat16 [2048, 1024], replicated, may hold values from -0.125 to 0.125
- critic_out: float32 [1024], replicated, may hold values from -0.1875 to 0.1875
Outputs:
- teacher_features: bfloat16 [4, 2048, 2, 2048], P('rep', 'expert')
- critic_logits: float32 [4, 2048, 2], P('rep', 'expert')
The draws below stay inside these ranges and needn't reach their ends.
Inputs may be any that keep to these rules, and one draw needn't show every extreme that they name: `expert_ids`: the 512 rows of one device name one expert at most 80 times in all, and some device reaches 80; the two experts of a token differ.
All inputs are finite; a program needn't handle non-finite values.
Results may differ from the reference program's by a relative error of at most 0.033.
Values may be sent and summed in bfloat16 or wider, within the bound.
No kernel may reach another device: no remote copies, remote signals or barrier semaphores. Data moves between devices by JAX's collectives and lax.ppermute only.
A program may use at most 192 MiB of HBM per device.

```python
import math
import jax
import jax.numpy as jnp
import numpy as np
from jax import lax

D = 2048
FF = 1408
HEADS = 16
SEQ = 2048
IMGS = 2
CRIT = 1024
HD = 128
EXPERTS = 16
TOK_DEV = 512
CAP = 80
N_EXPERT = 8
N_REP = 4


def draw_teacher_qkv(key, part):
    first, second, third = jax.random.split(jax.random.fold_in(key, 11), 3)
    scale = D ** (-0.5)
    query_part = jax.random.normal(first, (D, HEADS, HD), jnp.float32) * scale
    key_part = jax.random.normal(second, (D, HEADS, HD), jnp.float32) * scale
    value_part = jax.random.normal(third, (D, HEADS, HD), jnp.float32) * scale
    return jnp.stack([query_part, key_part, value_part], axis=1).astype(jnp.bfloat16)


def draw_qk_gain(key, part):
    first, second = jax.random.split(jax.random.fold_in(key, 23), 2)
    low_end, high_end = (math.log(0.7), math.log(2.0))
    head_scale = jnp.exp(jax.random.uniform(first, (2, HEADS, 1), jnp.float32, low_end, high_end))
    entry_scale = jax.random.uniform(second, (2, HEADS, HD), jnp.float32, 0.8, 1.2)
    return (head_scale * entry_scale).astype(jnp.float32)


def level_of(own_key, dims, cuts, low, top_value):
    level = 1.0
    for axis_at, blocks in cuts:
        heights = jax.random.uniform(jax.random.fold_in(jax.random.fold_in(own_key, 6), axis_at), (blocks,), jnp.float32, low / len(cuts), top_value / len(cuts))
        level = level * jnp.repeat(jnp.exp(heights), dims[axis_at] // blocks).reshape((-1,) + (1,) * (len(dims) - 1 - axis_at))
    return level


def shared_out(stream_key, own, number, rows, number_of, top, most, slope):
    sequence = jax.random.permutation(stream_key, number_of)
    heavy_load, common = portions_of(number_of, rows * top, most, slope, True), portions_of(number_of, rows * top, most, slope, False)
    places = jnp.arange(number_of)

    def named(sizes, turn):
        used = int((sizes > 0).sum())
        fixed = max(1, used // 4)
        shifted = fixed + (places - fixed + turn * (used - fixed)) % max(1, number_of - fixed)
        return jnp.zeros((number_of,), jnp.int32).at[sequence[jnp.where(places < fixed, places, shifted)]].set(jnp.asarray(sizes, jnp.int32))

    sizes = jnp.where(number % 4 == 0, named(heavy_load, number // 4), named(common, number - number // 4 - 1))
    mixed = jax.random.permutation(jax.random.fold_in(own, 3), number_of)
    giver, receiver = mixed[0:number_of // 2 * 2:2], mixed[1:number_of // 2 * 2:2]
    margin = jnp.minimum(sizes[giver] - 1, most - sizes[receiver]) // 2
    margin = jnp.where((giver == sequence[0]) | (receiver == sequence[0]) | (sizes[receiver] == 0), 0, jnp.maximum(margin, 0))
    shifted = jax.random.randint(jax.random.fold_in(own, 4), (number_of // 2,), 0, 1 << 20) % (margin + 1)
    sizes = sizes.at[giver].add(-shifted).at[receiver].add(shifted)
    labels = jnp.searchsorted(jnp.cumsum(sizes), jnp.arange(rows * top), side="right").astype(jnp.int32)
    grid = labels.reshape(top, rows).T
    grid = grid[jax.random.permutation(jax.random.fold_in(own, 1), rows)]
    turn = jax.random.randint(jax.random.fold_in(own, 2), (rows, 1), 0, top)
    return jnp.take_along_axis(grid, (jnp.arange(top)[None, :] + turn) % top, axis=1)


def portions_of(amount, total, most, skew, full):
    weights = [(1 << 20) // math.isqrt(grade ** skew) + 1 for grade in range(1, amount + 1)]
    largest = most if full else min(most, max(-(-total // amount), total * weights[0] // sum(weights)))
    least = 1 if total - largest >= amount - 1 else 0
    given, surplus = [largest] + [least] * (amount - 1), total - largest - least * (amount - 1)
    while surplus > 0:
        candidates = [i for i in range(1, amount) if given[i] < largest] or [i for i in range(1, amount) if given[i] < most]
        mass, budget = sum([weights[i] for i in candidates]), surplus
        for i in candidates:
            extra = min(most - given[i], max(1, budget * weights[i] // mass), surplus)
            given[i] = given[i] + extra
            surplus = surplus - extra
    return np.array(given)


def scatter_about(rng, shape, width, reach, cuts=(), held_as=jnp.bfloat16):
    result = jax.random.normal(rng, shape, jnp.float32) * width
    if len(cuts) > 0:
        result = level_of(rng, shape, cuts, -0.22, 0.18) * result
    return jnp.clip(result, min=-reach, max=reach).astype(held_as)


def setup_inputs(seed: int = 0) -> dict:
    streams_of = jax.random.split(jax.random.key(seed), 14)
    tokens = scatter_about(streams_of[0], (N_REP, SEQ, IMGS, D), 1.0, 6.0, ((0, 4), (1, 8)))
    expert_ids_keys = jax.random.split(jax.random.fold_in(streams_of[1], 1), N_REP * SEQ * IMGS // TOK_DEV)
    expert_ids_turns = jax.random.permutation(jax.random.fold_in(streams_of[1], 3), N_REP * SEQ * IMGS // TOK_DEV)
    expert_ids = jax.vmap(lambda own, number: shared_out(jax.random.fold_in(streams_of[1], 2), own, number, TOK_DEV, EXPERTS, 2, CAP, 1))(expert_ids_keys, expert_ids_turns).reshape((N_REP, SEQ, IMGS, 2))
    gate_probs = jnp.clip(jnp.exp(math.log(1.0) - 2.3025851 * jax.random.uniform(streams_of[2], (N_REP, SEQ, IMGS, 2), jnp.float32) ** level_of(streams_of[2], (N_REP, SEQ, IMGS, 2), ((0, 4), (1, 8)), -0.2, 0.2)), 0.1, 1.0)
    norm_gain = jnp.clip(1.0 + 0.15 * jax.random.normal(streams_of[3], (D,), jnp.float32), 0.25, 1.75)
    expert_gate = scatter_about(streams_of[4], (EXPERTS, D, FF), D ** -0.5, 0.125, ((0, 8), (2, 4)))
    expert_up = scatter_about(streams_of[5], (EXPERTS, D, FF), D ** -0.5, 0.125, ((0, 8), (2, 4)))
    expert_down = scatter_about(streams_of[6], (EXPERTS, FF, D), FF ** -0.5, 0.15625, ((0, 8), (1, 4)))
    teacher_gain = jnp.clip(1.0 + 0.15 * jax.random.normal(streams_of[7], (D,), jnp.float32), 0.25, 1.75)
    teacher_qkv = draw_teacher_qkv(jax.random.fold_in(streams_of[13], 71), 0)
    qk_gain = draw_qk_gain(jax.random.fold_in(streams_of[13], 71), 0)
    teacher_out = scatter_about(streams_of[10], (HEADS, HD, D), D ** -0.5, 0.125, ((0, 4),))
    critic_in = scatter_about(streams_of[11], (D, CRIT), D ** -0.5, 0.125)
    critic_out = scatter_about(streams_of[12], (CRIT,), CRIT ** -0.5, 0.1875, (), jnp.float32)
    return dict(tokens=tokens, expert_ids=expert_ids, gate_probs=gate_probs, norm_gain=norm_gain, expert_gate=expert_gate, expert_up=expert_up, expert_down=expert_down, teacher_gain=teacher_gain, teacher_qkv=teacher_qkv, qk_gain=qk_gain, teacher_out=teacher_out, critic_in=critic_in, critic_out=critic_out)


def norm_rows(values, gain):
    return values * lax.rsqrt(lax.optimization_barrier(jnp.mean(values * values, axis=-1, keepdims=True)) + 1e-06) * gain

def slot_numbers(chosen, count):
    onehot = (chosen[..., None] == jnp.arange(count, dtype=jnp.int32)).astype(jnp.int32)
    before = jnp.cumsum(onehot, axis=-2) - onehot
    return lax.optimization_barrier(jnp.sum(before * onehot, axis=-1)).astype(jnp.int32)

def run_expert(operands):
    rows, gate_w, up_w, down_w = operands
    gate_part = jnp.dot(rows, gate_w, preferred_element_type=jnp.float32)
    up_part = jnp.dot(rows, up_w, preferred_element_type=jnp.float32)
    hidden = (jax.nn.silu(gate_part) * up_part).astype(jnp.bfloat16)
    quarter = FF // N_REP
    total_sum = jnp.zeros((rows.shape[0], D), jnp.float32)
    for part_index in range(N_REP):
        low_edge = part_index * quarter
        partial_value = jnp.dot(hidden[:, low_edge:low_edge + quarter], down_w[low_edge:low_edge + quarter], preferred_element_type=jnp.float32).astype(jnp.bfloat16)
        partial_value = lax.optimization_barrier(partial_value)
        total_sum = total_sum + partial_value.astype(jnp.float32)
    return total_sum.astype(jnp.bfloat16)

def attend_pair(operands):
    query_rows, key_rows, value_rows = operands
    scores = jnp.dot(query_rows.astype(jnp.float32), key_rows.astype(jnp.float32).T, preferred_element_type=jnp.float32) * HD ** (-0.5)
    scores = scores - lax.optimization_barrier(jnp.max(scores, axis=-1, keepdims=True))
    weights = jnp.exp(scores)
    probs = (weights / lax.optimization_barrier(jnp.sum(weights, axis=-1, keepdims=True))).astype(jnp.bfloat16)
    return jnp.dot(probs, value_rows, preferred_element_type=jnp.float32).astype(jnp.bfloat16)

def reference(tokens, expert_ids, gate_probs, norm_gain, expert_gate, expert_up, expert_down, teacher_gain, teacher_qkv, qk_gain, teacher_out, critic_in, critic_out):
    residual = tokens.astype(jnp.float32).reshape(N_REP, N_EXPERT, TOK_DEV, D)
    normed = norm_rows(residual, norm_gain).astype(jnp.bfloat16)
    chosen = expert_ids.reshape(N_REP, N_EXPERT, 2 * TOK_DEV).astype(jnp.int32)
    slot_index = slot_numbers(chosen, EXPERTS)
    gate_value = gate_probs.astype(jnp.float32).reshape(N_REP, N_EXPERT, 2 * TOK_DEV)
    replica_pos = jnp.arange(N_REP, dtype=jnp.int32)[:, None, None]
    owner_pos = jnp.arange(N_EXPERT, dtype=jnp.int32)[None, :, None]
    row_index = ((replica_pos * N_EXPERT + owner_pos) * CAP + slot_index).astype(jnp.int32)
    token_of = (jnp.arange(2 * TOK_DEV, dtype=jnp.int32) // 2).astype(jnp.int32)
    source_rows = normed[:, :, token_of]
    buffer = jnp.zeros((EXPERTS, N_REP * N_EXPERT * CAP, D), jnp.bfloat16).at[chosen, row_index].set(source_rows)
    produced = lax.map(run_expert, (buffer, expert_gate, expert_up, expert_down))
    picked = produced[chosen, row_index].astype(jnp.float32) * gate_value[..., None]
    combined = picked.reshape(N_REP, N_EXPERT, TOK_DEV, 2, D).sum(axis=3)
    mixed = (residual + combined).astype(jnp.bfloat16).reshape(N_REP, SEQ, IMGS, D)

    def teach(block_in):
        teacher_in = norm_rows(block_in.astype(jnp.float32), teacher_gain).astype(jnp.bfloat16)
        projected = jnp.einsum('sid,djhe->jihse', teacher_in.astype(jnp.float32), teacher_qkv.astype(jnp.float32))
        query = norm_rows(projected[0], qk_gain[0][:, None, :]).astype(jnp.bfloat16)
        keyed = norm_rows(projected[1], qk_gain[1][:, None, :]).astype(jnp.bfloat16)
        valued = projected[2].astype(jnp.bfloat16)
        attended = lax.map(attend_pair, (query.reshape(IMGS * HEADS, SEQ, HD), keyed.reshape(IMGS * HEADS, SEQ, HD), valued.reshape(IMGS * HEADS, SEQ, HD)))
        attended = attended.reshape(IMGS, HEADS, SEQ, HD)
        heads_part = HEADS // N_REP
        total_sum = jnp.zeros((SEQ, IMGS, D), jnp.float32)
        for part_index in range(N_REP):
            low_edge = part_index * heads_part
            partial_value = jnp.einsum('ihse,hed->sid', attended[:, low_edge:low_edge + heads_part].astype(jnp.float32), teacher_out[low_edge:low_edge + heads_part].astype(jnp.float32)).astype(jnp.bfloat16)
            partial_value = lax.optimization_barrier(partial_value)
            total_sum = total_sum + partial_value.astype(jnp.float32)
        features = (block_in.astype(jnp.float32) + total_sum).astype(jnp.bfloat16)
        critic_hidden = jax.nn.gelu(jnp.dot(features.reshape(SEQ * IMGS, D), critic_in, preferred_element_type=jnp.float32), approximate=True)
        logits = jnp.dot(critic_hidden, critic_out, precision=lax.Precision.HIGHEST, preferred_element_type=jnp.float32)
        return (features, logits.reshape(SEQ, IMGS))
    teacher_features, critic_logits = lax.map(teach, mixed)
    return (teacher_features, critic_logits)
```

```python
import jax
import jax.numpy as jnp
from jax import lax
from jax.sharding import PartitionSpec as P


def norm_rows(values, gain):
    return values * lax.rsqrt(jnp.mean(values * values, axis=-1, keepdims=True) + 1e-06) * gain


def slot_numbers(chosen, count):
    onehot = (chosen[..., None] == jnp.arange(count, dtype=jnp.int32)).astype(jnp.int32)
    before = jnp.cumsum(onehot, axis=-2) - onehot
    return jnp.sum(before * onehot, axis=-1)


def local(
    tokens,
    expert_ids,
    gate_probs,
    norm_gain,
    expert_gate,
    expert_up,
    expert_down,
    teacher_gain,
    teacher_qkv,
    qk_gain,
    teacher_out,
    critic_in,
    critic_out,
):
    seq_dev = tokens.shape[1]
    images = tokens.shape[2]
    width = tokens.shape[3]
    tok_count = seq_dev * images
    n_owner = lax.axis_size("expert")
    n_replica = lax.axis_size("rep")
    exp_local = expert_gate.shape[0]
    expert_total = exp_local * n_owner
    capacity = max(2, tok_count * 10 // (4 * expert_total))
    gate_full = lax.all_gather(expert_gate, "rep", axis=2, tiled=True)
    up_full = lax.all_gather(expert_up, "rep", axis=2, tiled=True)
    down_full = lax.all_gather(expert_down, "rep", axis=1, tiled=True)
    qkv_full = lax.all_gather(teacher_qkv, "rep", axis=2, tiled=True)
    qk_gain_full = lax.all_gather(qk_gain, "rep", axis=1, tiled=True)
    out_full = lax.all_gather(teacher_out, "rep", axis=0, tiled=True)
    residual = tokens.reshape(tok_count, width).astype(jnp.float32)
    normed = norm_rows(residual, norm_gain).astype(jnp.bfloat16)
    chosen = expert_ids.reshape(2 * tok_count)
    slot_index = slot_numbers(chosen, expert_total)
    gate_value = gate_probs.reshape(2 * tok_count)
    target = chosen * capacity + slot_index
    token_of = jnp.arange(2 * tok_count, dtype=jnp.int32) // 2
    owner_token = jnp.zeros((expert_total * capacity,), jnp.int32).at[target].set(token_of)
    filled = jnp.zeros((expert_total * capacity,), jnp.bool_).at[target].set(True)
    outgoing = jnp.where(
        filled[:, None], jnp.take(normed, owner_token, axis=0), jnp.zeros((), jnp.bfloat16)
    )
    outgoing = outgoing.reshape(n_owner, exp_local * capacity, width)
    arrived = lax.all_to_all(outgoing, "expert", split_axis=0, concat_axis=0, tiled=True)
    arrived = arrived.reshape(n_owner, exp_local, capacity, width)
    gate_part = jnp.einsum(
        "sjcd,jdf->sjcf", arrived, gate_full, preferred_element_type=jnp.float32
    )
    up_part = jnp.einsum("sjcd,jdf->sjcf", arrived, up_full, preferred_element_type=jnp.float32)
    hidden = (jax.nn.silu(gate_part) * up_part).astype(jnp.bfloat16)
    ff_total = hidden.shape[-1]
    ff_part = ff_total // n_replica
    produced = jnp.zeros(arrived.shape, jnp.float32)
    for part in range(n_replica):
        low = part * ff_part
        produced = produced + jnp.einsum(
            "sjcf,jfd->sjcd",
            hidden[..., low:low + ff_part],
            down_full[:, low:low + ff_part],
            preferred_element_type=jnp.float32,
        ).astype(jnp.bfloat16).astype(jnp.float32)
    results = produced.astype(jnp.bfloat16).reshape(n_owner, exp_local * capacity, width)
    returned = lax.all_to_all(results, "expert", split_axis=0, concat_axis=0, tiled=True).reshape(
        expert_total * capacity, width
    )
    picked = jnp.take(returned, target, axis=0).astype(jnp.float32) * gate_value[:, None]
    combined = picked.reshape(tok_count, 2, width).sum(axis=1)
    mixed = (residual + combined).astype(jnp.bfloat16)
    teacher_in = norm_rows(mixed.astype(jnp.float32), teacher_gain).astype(jnp.bfloat16)
    teacher_in = teacher_in.reshape(seq_dev, images, width)
    heads_all = qkv_full.shape[2]
    head_size = qkv_full.shape[3]
    projected = jnp.einsum(
        "sid,djhe->jihse", teacher_in, qkv_full, preferred_element_type=jnp.float32
    )
    query = norm_rows(projected[0], qk_gain_full[0][:, None, :])
    keyed = norm_rows(projected[1], qk_gain_full[1][:, None, :])
    projected = jnp.stack([query, keyed, projected[2]]).astype(jnp.bfloat16)
    pairs_all = images * heads_all
    grouped = projected.reshape(3, pairs_all, seq_dev, head_size)
    whole = lax.all_to_all(grouped, "expert", split_axis=1, concat_axis=2, tiled=True)
    pairs_local = whole.shape[1]
    seq_len = whole.shape[2]
    block = min(512, seq_len)
    blocks_count = seq_len // block
    key_rows = whole[1]
    value_rows = whole[2]

    def attend(query_block):
        scores = jnp.einsum(
            "pqe,pke->pqk", query_block, key_rows, preferred_element_type=jnp.float32
        ) * head_size ** (-0.5)
        scores = scores - jnp.max(scores, axis=-1, keepdims=True)
        weights = jnp.exp(scores)
        probs = (weights / jnp.sum(weights, axis=-1, keepdims=True)).astype(jnp.bfloat16)
        return jnp.einsum(
            "pqk,pke->pqe", probs, value_rows, preferred_element_type=jnp.float32
        ).astype(jnp.bfloat16)

    query_blocks = (
        whole[0].reshape(pairs_local, blocks_count, block, head_size).transpose(1, 0, 2, 3)
    )
    attended = (
        lax.map(attend, query_blocks).transpose(1, 0, 2, 3).reshape(pairs_local, seq_len, head_size)
    )
    gathered_heads = lax.all_to_all(attended, "expert", split_axis=1, concat_axis=0, tiled=True)
    gathered_heads = gathered_heads.reshape(images, heads_all, seq_dev, head_size)
    heads_part = heads_all // n_replica
    projected_out = jnp.zeros((seq_dev, images, width), jnp.float32)
    for part in range(n_replica):
        low = part * heads_part
        projected_out = projected_out + jnp.einsum(
            "ihse,hed->sid",
            gathered_heads[:, low:low + heads_part],
            out_full[low:low + heads_part],
            preferred_element_type=jnp.float32,
        ).astype(jnp.bfloat16).astype(jnp.float32)
    features = (
        mixed.reshape(seq_dev, images, width).astype(jnp.float32) + projected_out
    ).astype(jnp.bfloat16)
    critic_hidden = jax.nn.gelu(
        jnp.dot(features.reshape(tok_count, width), critic_in, preferred_element_type=jnp.float32),
        approximate=True,
    )
    logits = jnp.dot(
        critic_hidden,
        critic_out,
        precision=lax.Precision.HIGHEST,
        preferred_element_type=jnp.float32,
    )
    return (features.reshape(1, seq_dev, images, width), logits.reshape(1, seq_dev, images))


def solution(mesh):
    return jax.shard_map(
        local,
        mesh=mesh,
        in_specs=(
            P("rep", "expert", None, None),
            P("rep", "expert", None, None),
            P("rep", "expert", None, None),
            P(),
            P("expert", None, "rep"),
            P("expert", None, "rep"),
            P("expert", "rep", None),
            P(),
            P(None, None, "rep", None),
            P(None, "rep", None),
            P("rep", None, None),
            P(),
            P(),
        ),
        out_specs=(P("rep", "expert", None, None), P("rep", "expert", None)),
        check_vma=False,
    )
```

```python
import functools

import jax
import jax.numpy as jnp
from jax import lax
from jax.experimental import pallas as pl
from jax.sharding import PartitionSpec as P


def norm_rows(values, gain):
    return values * lax.rsqrt(jnp.mean(values * values, axis=-1, keepdims=True) + 1e-06) * gain


def slot_numbers(chosen, count):
    onehot = (chosen[..., None] == jnp.arange(count, dtype=jnp.int32)).astype(jnp.int32)
    before = jnp.cumsum(onehot, axis=-2) - onehot
    return jnp.sum(before * onehot, axis=-1)


def attention_kernel(query_ref, key_ref, value_ref, out_ref, *, scale):
    scores = lax.dot_general(
        query_ref[...],
        key_ref[...],
        (((1,), (1,)), ((), ())),
        preferred_element_type=jnp.float32,
    ) * scale
    scores = scores - jnp.max(scores, axis=-1, keepdims=True)
    weights = jnp.exp(scores)
    probs = (weights / jnp.sum(weights, axis=-1, keepdims=True)).astype(jnp.bfloat16)
    out_ref[...] = jnp.dot(probs, value_ref[...], preferred_element_type=jnp.float32).astype(
        out_ref.dtype
    )


def attention(whole, scale, interpret=False):
    _, pairs, seq_len, head_size = whole.shape
    block = min(256, seq_len)
    return pl.pallas_call(
        functools.partial(attention_kernel, scale=scale),
        grid=(pairs, seq_len // block),
        in_specs=[
            pl.BlockSpec((None, None, block, head_size), lambda p, i: (0, p, i, 0)),
            pl.BlockSpec((None, None, seq_len, head_size), lambda p, i: (1, p, 0, 0)),
            pl.BlockSpec((None, None, seq_len, head_size), lambda p, i: (2, p, 0, 0)),
        ],
        out_specs=pl.BlockSpec((None, block, head_size), lambda p, i: (p, i, 0)),
        out_shape=jax.ShapeDtypeStruct((pairs, seq_len, head_size), whole.dtype),
        interpret=interpret,
    )(whole, whole, whole)


def local(
    tokens,
    expert_ids,
    gate_probs,
    norm_gain,
    expert_gate,
    expert_up,
    expert_down,
    teacher_gain,
    teacher_qkv,
    qk_gain,
    teacher_out,
    critic_in,
    critic_out,
):
    seq_dev = tokens.shape[1]
    images = tokens.shape[2]
    width = tokens.shape[3]
    tok_count = seq_dev * images
    n_owner = lax.axis_size("expert")
    n_replica = lax.axis_size("rep")
    exp_local = expert_gate.shape[0]
    expert_total = exp_local * n_owner
    capacity = max(2, tok_count * 10 // (4 * expert_total))
    gate_full = lax.all_gather(expert_gate, "rep", axis=2, tiled=True)
    up_full = lax.all_gather(expert_up, "rep", axis=2, tiled=True)
    down_full = lax.all_gather(expert_down, "rep", axis=1, tiled=True)
    qkv_full = lax.all_gather(teacher_qkv, "rep", axis=2, tiled=True)
    qk_gain_full = lax.all_gather(qk_gain, "rep", axis=1, tiled=True)
    out_full = lax.all_gather(teacher_out, "rep", axis=0, tiled=True)
    residual = tokens.reshape(tok_count, width).astype(jnp.float32)
    normed = norm_rows(residual, norm_gain).astype(jnp.bfloat16)
    chosen = expert_ids.reshape(2 * tok_count)
    slot_index = slot_numbers(chosen, expert_total)
    gate_value = gate_probs.reshape(2 * tok_count)
    target = chosen * capacity + slot_index
    token_of = jnp.arange(2 * tok_count, dtype=jnp.int32) // 2
    owner_token = jnp.zeros((expert_total * capacity,), jnp.int32).at[target].set(token_of)
    filled = jnp.zeros((expert_total * capacity,), jnp.bool_).at[target].set(True)
    outgoing = jnp.where(
        filled[:, None], jnp.take(normed, owner_token, axis=0), jnp.zeros((), jnp.bfloat16)
    )
    outgoing = outgoing.reshape(n_owner, exp_local * capacity, width)
    arrived = lax.all_to_all(outgoing, "expert", split_axis=0, concat_axis=0, tiled=True)
    arrived = arrived.reshape(n_owner, exp_local, capacity, width)
    gate_part = jnp.einsum(
        "sjcd,jdf->sjcf", arrived, gate_full, preferred_element_type=jnp.float32
    )
    up_part = jnp.einsum("sjcd,jdf->sjcf", arrived, up_full, preferred_element_type=jnp.float32)
    hidden = (jax.nn.silu(gate_part) * up_part).astype(jnp.bfloat16)
    ff_total = hidden.shape[-1]
    ff_part = ff_total // n_replica
    produced = jnp.zeros(arrived.shape, jnp.float32)
    for part in range(n_replica):
        low = part * ff_part
        produced = produced + jnp.einsum(
            "sjcf,jfd->sjcd",
            hidden[..., low:low + ff_part],
            down_full[:, low:low + ff_part],
            preferred_element_type=jnp.float32,
        ).astype(jnp.bfloat16).astype(jnp.float32)
    results = produced.astype(jnp.bfloat16).reshape(n_owner, exp_local * capacity, width)
    returned = lax.all_to_all(results, "expert", split_axis=0, concat_axis=0, tiled=True).reshape(
        expert_total * capacity, width
    )
    picked = jnp.take(returned, target, axis=0).astype(jnp.float32) * gate_value[:, None]
    combined = picked.reshape(tok_count, 2, width).sum(axis=1)
    mixed = (residual + combined).astype(jnp.bfloat16)
    teacher_in = norm_rows(mixed.astype(jnp.float32), teacher_gain).astype(jnp.bfloat16)
    teacher_in = teacher_in.reshape(seq_dev, images, width)
    heads_all = qkv_full.shape[2]
    head_size = qkv_full.shape[3]
    projected = jnp.einsum(
        "sid,djhe->jihse", teacher_in, qkv_full, preferred_element_type=jnp.float32
    )
    query = norm_rows(projected[0], qk_gain_full[0][:, None, :])
    keyed = norm_rows(projected[1], qk_gain_full[1][:, None, :])
    projected = jnp.stack([query, keyed, projected[2]]).astype(jnp.bfloat16)
    pairs_all = images * heads_all
    grouped = projected.reshape(3, pairs_all, seq_dev, head_size)
    whole = lax.all_to_all(grouped, "expert", split_axis=1, concat_axis=2, tiled=True)
    pairs_local = whole.shape[1]
    seq_len = whole.shape[2]
    attended = attention(whole, head_size ** (-0.5))
    gathered_heads = lax.all_to_all(attended, "expert", split_axis=1, concat_axis=0, tiled=True)
    gathered_heads = gathered_heads.reshape(images, heads_all, seq_dev, head_size)
    heads_part = heads_all // n_replica
    projected_out = jnp.zeros((seq_dev, images, width), jnp.float32)
    for part in range(n_replica):
        low = part * heads_part
        projected_out = projected_out + jnp.einsum(
            "ihse,hed->sid",
            gathered_heads[:, low:low + heads_part],
            out_full[low:low + heads_part],
            preferred_element_type=jnp.float32,
        ).astype(jnp.bfloat16).astype(jnp.float32)
    features = (
        mixed.reshape(seq_dev, images, width).astype(jnp.float32) + projected_out
    ).astype(jnp.bfloat16)
    critic_hidden = jax.nn.gelu(
        jnp.dot(features.reshape(tok_count, width), critic_in, preferred_element_type=jnp.float32),
        approximate=True,
    )
    logits = jnp.dot(
        critic_hidden,
        critic_out,
        precision=lax.Precision.HIGHEST,
        preferred_element_type=jnp.float32,
    )
    return (features.reshape(1, seq_dev, images, width), logits.reshape(1, seq_dev, images))


def solution(mesh):
    return jax.shard_map(
        local,
        mesh=mesh,
        in_specs=(
            P("rep", "expert", None, None),
            P("rep", "expert", None, None),
            P("rep", "expert", None, None),
            P(),
            P("expert", None, "rep"),
            P("expert", None, "rep"),
            P("expert", "rep", None),
            P(),
            P(None, None, "rep", None),
            P(None, "rep", None),
            P("rep", None, None),
            P(),
            P(),
        ),
        out_specs=(P("rep", "expert", None, None), P("rep", "expert", None)),
        check_vma=False,
    )
```

```python
import functools

import jax
import jax.numpy as jnp
from jax import lax
from jax.experimental import pallas as pl
from jax.sharding import PartitionSpec as P


def norm_rows(values, gain):
    return values * lax.rsqrt(jnp.mean(values * values, axis=-1, keepdims=True) + 1e-06) * gain


def slot_numbers(chosen, count):
    onehot = (chosen[..., None] == jnp.arange(count, dtype=jnp.int32)).astype(jnp.int32)
    before = jnp.cumsum(onehot, axis=-2) - onehot
    return jnp.sum(before * onehot, axis=-1)


def attention_kernel(query_ref, key_ref, value_ref, out_ref, *, scale):
    scores = lax.dot_general(
        query_ref[...],
        key_ref[...],
        (((1,), (1,)), ((), ())),
        preferred_element_type=jnp.float32,
    ) * scale
    scores = scores - jnp.max(scores, axis=-1, keepdims=True)
    weights = jnp.exp(scores)
    probs = (weights / jnp.sum(weights, axis=-1, keepdims=True)).astype(jnp.bfloat16)
    out_ref[...] = jnp.dot(probs, value_ref[...], preferred_element_type=jnp.float32).astype(
        out_ref.dtype
    )


def attention(whole, scale, interpret=False):
    _, pairs, seq_len, head_size = whole.shape
    block = min(256, seq_len)
    return pl.pallas_call(
        functools.partial(attention_kernel, scale=scale),
        grid=(pairs, seq_len // block),
        in_specs=[
            pl.BlockSpec((None, None, block, head_size), lambda p, i: (0, p, i, 0)),
            pl.BlockSpec((None, None, seq_len, head_size), lambda p, i: (1, p, 0, 0)),
            pl.BlockSpec((None, None, seq_len, head_size), lambda p, i: (2, p, 0, 0)),
        ],
        out_specs=pl.BlockSpec((None, block, head_size), lambda p, i: (p, i, 0)),
        out_shape=jax.ShapeDtypeStruct((pairs, seq_len, head_size), whole.dtype),
        interpret=interpret,
    )(whole, whole, whole)


def local(
    tokens,
    expert_ids,
    gate_probs,
    norm_gain,
    expert_gate,
    expert_up,
    expert_down,
    teacher_gain,
    teacher_qkv,
    qk_gain,
    teacher_out,
    critic_in,
    critic_out,
):
    seq_dev = tokens.shape[1]
    images = tokens.shape[2]
    width = tokens.shape[3]
    tok_count = seq_dev * images
    n_owner = lax.axis_size("expert")
    n_replica = lax.axis_size("rep")
    exp_local = expert_gate.shape[0]
    expert_total = exp_local * n_owner
    capacity = max(2, tok_count * 10 // (4 * expert_total))
    gate_full = lax.all_gather(expert_gate, "rep", axis=2, tiled=True)
    up_full = lax.all_gather(expert_up, "rep", axis=2, tiled=True)
    down_full = lax.all_gather(expert_down, "rep", axis=1, tiled=True)
    qkv_full = lax.all_gather(teacher_qkv, "rep", axis=2, tiled=True)
    qk_gain_full = lax.all_gather(qk_gain, "rep", axis=1, tiled=True)
    out_full = lax.all_gather(teacher_out, "rep", axis=0, tiled=True)
    residual = tokens.reshape(tok_count, width).astype(jnp.float32)
    normed = norm_rows(residual, norm_gain).astype(jnp.bfloat16)
    chosen = expert_ids.reshape(2 * tok_count)
    slot_index = slot_numbers(chosen, expert_total)
    gate_value = gate_probs.reshape(2 * tok_count)
    target = chosen * capacity + slot_index
    rows_all = jnp.arange(expert_total * capacity, dtype=jnp.int32)
    assign_rows = (target[:, None] == rows_all[None, :]).astype(jnp.bfloat16)
    token_rows = assign_rows.reshape(tok_count, 2, expert_total * capacity).sum(axis=1)
    outgoing = jnp.einsum(
        "tr,td->rd", token_rows, normed, preferred_element_type=jnp.float32
    ).astype(jnp.bfloat16)
    outgoing = outgoing.reshape(n_owner, exp_local * capacity, width)
    arrived = lax.all_to_all(outgoing, "expert", split_axis=0, concat_axis=0, tiled=True)
    arrived = arrived.reshape(n_owner, exp_local, capacity, width)
    gate_part = jnp.einsum(
        "sjcd,jdf->sjcf", arrived, gate_full, preferred_element_type=jnp.float32
    )
    up_part = jnp.einsum("sjcd,jdf->sjcf", arrived, up_full, preferred_element_type=jnp.float32)
    hidden = (jax.nn.silu(gate_part) * up_part).astype(jnp.bfloat16)
    ff_total = hidden.shape[-1]
    ff_part = ff_total // n_replica
    produced = jnp.zeros(arrived.shape, jnp.float32)
    for part in range(n_replica):
        low = part * ff_part
        produced = produced + jnp.einsum(
            "sjcf,jfd->sjcd",
            hidden[..., low:low + ff_part],
            down_full[:, low:low + ff_part],
            preferred_element_type=jnp.float32,
        ).astype(jnp.bfloat16).astype(jnp.float32)
    results = produced.astype(jnp.bfloat16).reshape(n_owner, exp_local * capacity, width)
    returned = lax.all_to_all(results, "expert", split_axis=0, concat_axis=0, tiled=True).reshape(
        expert_total * capacity, width
    )
    picked = jnp.dot(assign_rows, returned, preferred_element_type=jnp.float32) * gate_value[:, None]
    combined = picked.reshape(tok_count, 2, width).sum(axis=1)
    mixed = (residual + combined).astype(jnp.bfloat16)
    teacher_in = norm_rows(mixed.astype(jnp.float32), teacher_gain).astype(jnp.bfloat16)
    teacher_in = teacher_in.reshape(seq_dev, images, width)
    heads_all = qkv_full.shape[2]
    head_size = qkv_full.shape[3]
    projected = jnp.einsum(
        "sid,djhe->jihse", teacher_in, qkv_full, preferred_element_type=jnp.float32
    )
    query = norm_rows(projected[0], qk_gain_full[0][:, None, :])
    keyed = norm_rows(projected[1], qk_gain_full[1][:, None, :])
    projected = jnp.stack([query, keyed, projected[2]]).astype(jnp.bfloat16)
    pairs_all = images * heads_all
    grouped = projected.reshape(3, pairs_all, seq_dev, head_size)
    whole = lax.all_to_all(grouped, "expert", split_axis=1, concat_axis=2, tiled=True)
    pairs_local = whole.shape[1]
    seq_len = whole.shape[2]
    attended = attention(whole, head_size ** (-0.5))
    gathered_heads = lax.all_to_all(attended, "expert", split_axis=1, concat_axis=0, tiled=True)
    gathered_heads = gathered_heads.reshape(images, heads_all, seq_dev, head_size)
    heads_part = heads_all // n_replica
    projected_out = jnp.zeros((seq_dev, images, width), jnp.float32)
    for part in range(n_replica):
        low = part * heads_part
        projected_out = projected_out + jnp.einsum(
            "ihse,hed->sid",
            gathered_heads[:, low:low + heads_part],
            out_full[low:low + heads_part],
            preferred_element_type=jnp.float32,
        ).astype(jnp.bfloat16).astype(jnp.float32)
    features = (
        mixed.reshape(seq_dev, images, width).astype(jnp.float32) + projected_out
    ).astype(jnp.bfloat16)
    critic_hidden = jax.nn.gelu(
        jnp.dot(features.reshape(tok_count, width), critic_in, preferred_element_type=jnp.float32),
        approximate=True,
    )
    logits = jnp.dot(
        critic_hidden,
        critic_out,
        precision=lax.Precision.HIGHEST,
        preferred_element_type=jnp.float32,
    )
    return (features.reshape(1, seq_dev, images, width), logits.reshape(1, seq_dev, images))


def solution(mesh):
    return jax.shard_map(
        local,
        mesh=mesh,
        in_specs=(
            P("rep", "expert", None, None),
            P("rep", "expert", None, None),
            P("rep", "expert", None, None),
            P(),
            P("expert", None, "rep"),
            P("expert", None, "rep"),
            P("expert", "rep", None),
            P(),
            P(None, None, "rep", None),
            P(None, "rep", None),
            P("rep", None, None),
            P(),
            P(),
        ),
        out_specs=(P("rep", "expert", None, None), P("rep", "expert", None)),
        check_vma=False,
    )
```

```python
import functools

import jax
import jax.numpy as jnp
from jax import lax
from jax.experimental import pallas as pl
from jax.sharding import PartitionSpec as P


def norm_rows(values, gain):
    return values * lax.rsqrt(jnp.mean(values * values, axis=-1, keepdims=True) + 1e-06) * gain


def slot_numbers(chosen, count):
    onehot = (chosen[..., None] == jnp.arange(count, dtype=jnp.int32)).astype(jnp.int32)
    before = jnp.cumsum(onehot, axis=-2) - onehot
    return jnp.sum(before * onehot, axis=-1)


def attention_kernel(query_ref, key_ref, value_ref, out_ref, *, scale):
    scores = lax.dot_general(
        query_ref[...],
        key_ref[...],
        (((1,), (1,)), ((), ())),
        preferred_element_type=jnp.float32,
    ) * scale
    scores = scores - jnp.max(scores, axis=-1, keepdims=True)
    weights = jnp.exp(scores)
    probs = (weights / jnp.sum(weights, axis=-1, keepdims=True)).astype(jnp.bfloat16)
    out_ref[...] = jnp.dot(probs, value_ref[...], preferred_element_type=jnp.float32).astype(
        out_ref.dtype
    )


def attention(whole, scale, interpret=False):
    _, pairs, seq_len, head_size = whole.shape
    block = min(256, seq_len)
    return pl.pallas_call(
        functools.partial(attention_kernel, scale=scale),
        grid=(pairs, seq_len // block),
        in_specs=[
            pl.BlockSpec((None, None, block, head_size), lambda p, i: (0, p, i, 0)),
            pl.BlockSpec((None, None, seq_len, head_size), lambda p, i: (1, p, 0, 0)),
            pl.BlockSpec((None, None, seq_len, head_size), lambda p, i: (2, p, 0, 0)),
        ],
        out_specs=pl.BlockSpec((None, block, head_size), lambda p, i: (p, i, 0)),
        out_shape=jax.ShapeDtypeStruct((pairs, seq_len, head_size), whole.dtype),
        interpret=interpret,
    )(whole, whole, whole)


def rep_parts(parts, count):
    if count == 1:
        return [parts]

    def send(values, shift):
        return tuple(
            lax.ppermute(v, "rep", [(i, shift(i)) for i in range(count)]) for v in values
        )

    if count == 4:
        far = send(parts, lambda i: i ^ 2)
        near = send(parts, lambda i: i ^ 1)
        far_near = send(far, lambda i: i ^ 1)
        return [parts, near, far, far_near]
    received = [parts]
    for _ in range(count - 1):
        received.append(send(received[-1], lambda i: (i + 1) % count))
    return received


def local(
    tokens,
    expert_ids,
    gate_probs,
    norm_gain,
    expert_gate,
    expert_up,
    expert_down,
    teacher_gain,
    teacher_qkv,
    qk_gain,
    teacher_out,
    critic_in,
    critic_out,
):
    seq_dev = tokens.shape[1]
    images = tokens.shape[2]
    width = tokens.shape[3]
    tok_count = seq_dev * images
    n_owner = lax.axis_size("expert")
    n_replica = lax.axis_size("rep")
    exp_local = expert_gate.shape[0]
    expert_total = exp_local * n_owner
    capacity = max(2, tok_count * 10 // (4 * expert_total))
    weight_parts = rep_parts((expert_gate, expert_up, expert_down), n_replica)
    qkv_full = lax.all_gather(teacher_qkv, "rep", axis=2, tiled=True)
    qk_gain_full = lax.all_gather(qk_gain, "rep", axis=1, tiled=True)
    out_full = lax.all_gather(teacher_out, "rep", axis=0, tiled=True)
    residual = tokens.reshape(tok_count, width).astype(jnp.float32)
    normed = norm_rows(residual, norm_gain).astype(jnp.bfloat16)
    chosen = expert_ids.reshape(2 * tok_count)
    slot_index = slot_numbers(chosen, expert_total)
    gate_value = gate_probs.reshape(2 * tok_count)
    target = chosen * capacity + slot_index
    rows_all = jnp.arange(expert_total * capacity, dtype=jnp.int32)
    assign_rows = (target[:, None] == rows_all[None, :]).astype(jnp.bfloat16)
    token_rows = assign_rows.reshape(tok_count, 2, expert_total * capacity).sum(axis=1)
    outgoing = jnp.einsum(
        "tr,td->rd", token_rows, normed, preferred_element_type=jnp.float32
    ).astype(jnp.bfloat16)
    outgoing = outgoing.reshape(n_owner, exp_local * capacity, width)
    arrived = lax.all_to_all(outgoing, "expert", split_axis=0, concat_axis=0, tiled=True)
    arrived = arrived.reshape(n_owner, exp_local, capacity, width)
    produced = jnp.zeros(arrived.shape, jnp.float32)
    for gate_w, up_w, down_w in weight_parts:
        gate_part = jnp.einsum(
            "sjcd,jdf->sjcf", arrived, gate_w, preferred_element_type=jnp.float32
        )
        up_part = jnp.einsum("sjcd,jdf->sjcf", arrived, up_w, preferred_element_type=jnp.float32)
        hidden = (jax.nn.silu(gate_part) * up_part).astype(jnp.bfloat16)
        produced = produced + jnp.einsum(
            "sjcf,jfd->sjcd", hidden, down_w, preferred_element_type=jnp.float32
        ).astype(jnp.bfloat16).astype(jnp.float32)
    results = produced.astype(jnp.bfloat16).reshape(n_owner, exp_local * capacity, width)
    returned = lax.all_to_all(results, "expert", split_axis=0, concat_axis=0, tiled=True).reshape(
        expert_total * capacity, width
    )
    picked = jnp.dot(assign_rows, returned, preferred_element_type=jnp.float32) * gate_value[:, None]
    combined = picked.reshape(tok_count, 2, width).sum(axis=1)
    mixed = (residual + combined).astype(jnp.bfloat16)
    teacher_in = norm_rows(mixed.astype(jnp.float32), teacher_gain).astype(jnp.bfloat16)
    teacher_in = teacher_in.reshape(seq_dev, images, width)
    heads_all = qkv_full.shape[2]
    head_size = qkv_full.shape[3]
    projected = jnp.einsum(
        "sid,djhe->jihse", teacher_in, qkv_full, preferred_element_type=jnp.float32
    )
    query = norm_rows(projected[0], qk_gain_full[0][:, None, :])
    keyed = norm_rows(projected[1], qk_gain_full[1][:, None, :])
    projected = jnp.stack([query, keyed, projected[2]]).astype(jnp.bfloat16)
    pairs_all = images * heads_all
    grouped = projected.reshape(3, pairs_all, seq_dev, head_size)
    whole = lax.all_to_all(grouped, "expert", split_axis=1, concat_axis=2, tiled=True)
    pairs_local = whole.shape[1]
    seq_len = whole.shape[2]
    attended = attention(whole, head_size ** (-0.5))
    gathered_heads = lax.all_to_all(attended, "expert", split_axis=1, concat_axis=0, tiled=True)
    gathered_heads = gathered_heads.reshape(images, heads_all, seq_dev, head_size)
    heads_part = heads_all // n_replica
    projected_out = jnp.zeros((seq_dev, images, width), jnp.float32)
    for part in range(n_replica):
        low = part * heads_part
        projected_out = projected_out + jnp.einsum(
            "ihse,hed->sid",
            gathered_heads[:, low:low + heads_part],
            out_full[low:low + heads_part],
            preferred_element_type=jnp.float32,
        ).astype(jnp.bfloat16).astype(jnp.float32)
    features = (
        mixed.reshape(seq_dev, images, width).astype(jnp.float32) + projected_out
    ).astype(jnp.bfloat16)
    critic_hidden = jax.nn.gelu(
        jnp.dot(features.reshape(tok_count, width), critic_in, preferred_element_type=jnp.float32),
        approximate=True,
    )
    logits = jnp.dot(
        critic_hidden,
        critic_out,
        precision=lax.Precision.HIGHEST,
        preferred_element_type=jnp.float32,
    )
    return (features.reshape(1, seq_dev, images, width), logits.reshape(1, seq_dev, images))


def solution(mesh):
    return jax.shard_map(
        local,
        mesh=mesh,
        in_specs=(
            P("rep", "expert", None, None),
            P("rep", "expert", None, None),
            P("rep", "expert", None, None),
            P(),
            P("expert", None, "rep"),
            P("expert", None, "rep"),
            P("expert", "rep", None),
            P(),
            P(None, None, "rep", None),
            P(None, "rep", None),
            P("rep", None, None),
            P(),
            P(),
        ),
        out_specs=(P("rep", "expert", None, None), P("rep", "expert", None)),
        check_vma=False,
    )
```

```python
import functools

import jax
import jax.numpy as jnp
from jax import lax
from jax.experimental import pallas as pl
from jax.sharding import PartitionSpec as P


def norm_rows(values, gain):
    return values * lax.rsqrt(jnp.mean(values * values, axis=-1, keepdims=True) + 1e-06) * gain


def slot_numbers(chosen, count):
    onehot = (chosen[..., None] == jnp.arange(count, dtype=jnp.int32)).astype(jnp.int32)
    before = jnp.cumsum(onehot, axis=-2) - onehot
    return jnp.sum(before * onehot, axis=-1)


def attention_kernel(query_ref, key_ref, value_ref, out_ref, *, scale):
    scores = lax.dot_general(
        query_ref[...],
        key_ref[...],
        (((1,), (1,)), ((), ())),
        preferred_element_type=jnp.float32,
    ) * scale
    scores = scores - jnp.max(scores, axis=-1, keepdims=True)
    weights = jnp.exp(scores)
    probs = (weights / jnp.sum(weights, axis=-1, keepdims=True)).astype(jnp.bfloat16)
    out_ref[...] = jnp.dot(probs, value_ref[...], preferred_element_type=jnp.float32).astype(
        out_ref.dtype
    )


def attention(whole, scale, interpret=False):
    _, pairs, seq_len, head_size = whole.shape
    block = min(256, seq_len)
    return pl.pallas_call(
        functools.partial(attention_kernel, scale=scale),
        grid=(pairs, seq_len // block),
        in_specs=[
            pl.BlockSpec((None, None, block, head_size), lambda p, i: (0, p, i, 0)),
            pl.BlockSpec((None, None, seq_len, head_size), lambda p, i: (1, p, 0, 0)),
            pl.BlockSpec((None, None, seq_len, head_size), lambda p, i: (2, p, 0, 0)),
        ],
        out_specs=pl.BlockSpec((None, block, head_size), lambda p, i: (p, i, 0)),
        out_shape=jax.ShapeDtypeStruct((pairs, seq_len, head_size), whole.dtype),
        interpret=interpret,
    )(whole, whole, whole)


def local(
    tokens,
    expert_ids,
    gate_probs,
    norm_gain,
    expert_gate,
    expert_up,
    expert_down,
    teacher_gain,
    teacher_qkv,
    qk_gain,
    teacher_out,
    critic_in,
    critic_out,
):
    seq_dev = tokens.shape[1]
    images = tokens.shape[2]
    width = tokens.shape[3]
    tok_count = seq_dev * images
    n_owner = lax.axis_size("expert")
    n_replica = lax.axis_size("rep")
    exp_local = expert_gate.shape[0]
    expert_total = exp_local * n_owner
    capacity = max(2, tok_count * 10 // (4 * expert_total))
    gate_full = lax.all_gather(expert_gate, "rep", axis=2, tiled=True)
    up_full = lax.all_gather(expert_up, "rep", axis=2, tiled=True)
    down_full = lax.all_gather(expert_down, "rep", axis=1, tiled=True)
    qkv_full = lax.all_gather(teacher_qkv, "rep", axis=2, tiled=True)
    qk_gain_full = lax.all_gather(qk_gain, "rep", axis=1, tiled=True)
    out_full = lax.all_gather(teacher_out, "rep", axis=0, tiled=True)
    residual = tokens.reshape(tok_count, width).astype(jnp.float32)
    normed = norm_rows(residual, norm_gain).astype(jnp.bfloat16)
    chosen = expert_ids.reshape(2 * tok_count)
    slot_index = slot_numbers(chosen, expert_total)
    gate_value = gate_probs.reshape(2 * tok_count)
    target = chosen * capacity + slot_index
    rows_all = jnp.arange(expert_total * capacity, dtype=jnp.int32)
    assign_rows = (target[:, None] == rows_all[None, :]).astype(jnp.bfloat16)
    token_rows = assign_rows.reshape(tok_count, 2, expert_total * capacity).sum(axis=1)
    outgoing = jnp.einsum(
        "tr,td->rd", token_rows, normed, preferred_element_type=jnp.float32
    ).astype(jnp.bfloat16)
    outgoing = outgoing.reshape(n_owner, exp_local * capacity, width)
    arrived = lax.all_to_all(outgoing, "expert", split_axis=0, concat_axis=0, tiled=True)
    arrived = arrived.reshape(n_owner, exp_local, capacity, width)
    gate_part = jnp.einsum(
        "sjcd,jdf->sjcf", arrived, gate_full, preferred_element_type=jnp.float32
    )
    up_part = jnp.einsum("sjcd,jdf->sjcf", arrived, up_full, preferred_element_type=jnp.float32)
    hidden = (jax.nn.silu(gate_part) * up_part).astype(jnp.bfloat16)
    ff_total = hidden.shape[-1]
    ff_part = ff_total // n_replica
    produced = jnp.zeros(arrived.shape, jnp.float32)
    for part in range(n_replica):
        low = part * ff_part
        produced = produced + jnp.einsum(
            "sjcf,jfd->sjcd",
            hidden[..., low:low + ff_part],
            down_full[:, low:low + ff_part],
            preferred_element_type=jnp.float32,
        ).astype(jnp.bfloat16).astype(jnp.float32)
    results = produced.astype(jnp.bfloat16).reshape(n_owner, exp_local * capacity, width)
    returned = lax.all_to_all(results, "expert", split_axis=0, concat_axis=0, tiled=True).reshape(
        expert_total * capacity, width
    )
    picked = jnp.dot(assign_rows, returned, preferred_element_type=jnp.float32) * gate_value[:, None]
    combined = picked.reshape(tok_count, 2, width).sum(axis=1)
    mixed = (residual + combined).astype(jnp.bfloat16)
    teacher_in = norm_rows(mixed.astype(jnp.float32), teacher_gain).astype(jnp.bfloat16)
    teacher_in = teacher_in.reshape(seq_dev, images, width)
    mixed = mixed.reshape(seq_dev, images, width)
    heads_all = qkv_full.shape[2]
    head_size = qkv_full.shape[3]
    chunks = images if (heads_all % n_owner == 0) else 1
    per_chunk = images // chunks
    features_parts = []
    logits_parts = []
    for chunk in range(chunks):
        sel = slice(chunk * per_chunk, (chunk + 1) * per_chunk)
        features, logits = teach(
            teacher_in[:, sel], mixed[:, sel], qkv_full, qk_gain_full, out_full, critic_in, critic_out,
            n_replica,
        )
        features_parts.append(features)
        logits_parts.append(logits)
    features = jnp.concatenate(features_parts, axis=1)
    logits = jnp.concatenate(logits_parts, axis=1)
    return (features.reshape(1, seq_dev, images, width), logits.reshape(1, seq_dev, images))


def teach(teacher_in, mixed, qkv_full, qk_gain_full, out_full, critic_in, critic_out, n_replica):
    seq_dev, images, width = teacher_in.shape
    heads_all = qkv_full.shape[2]
    head_size = qkv_full.shape[3]
    projected = jnp.einsum(
        "sid,djhe->jihse", teacher_in, qkv_full, preferred_element_type=jnp.float32
    )
    query = norm_rows(projected[0], qk_gain_full[0][:, None, :])
    keyed = norm_rows(projected[1], qk_gain_full[1][:, None, :])
    projected = jnp.stack([query, keyed, projected[2]]).astype(jnp.bfloat16)
    pairs_all = images * heads_all
    grouped = projected.reshape(3, pairs_all, seq_dev, head_size)
    whole = lax.all_to_all(grouped, "expert", split_axis=1, concat_axis=2, tiled=True)
    attended = attention(whole, head_size ** (-0.5))
    gathered_heads = lax.all_to_all(attended, "expert", split_axis=1, concat_axis=0, tiled=True)
    gathered_heads = gathered_heads.reshape(images, heads_all, seq_dev, head_size)
    heads_part = heads_all // n_replica
    projected_out = jnp.zeros((seq_dev, images, width), jnp.float32)
    for part in range(n_replica):
        low = part * heads_part
        projected_out = projected_out + jnp.einsum(
            "ihse,hed->sid",
            gathered_heads[:, low:low + heads_part],
            out_full[low:low + heads_part],
            preferred_element_type=jnp.float32,
        ).astype(jnp.bfloat16).astype(jnp.float32)
    features = (mixed.astype(jnp.float32) + projected_out).astype(jnp.bfloat16)
    critic_hidden = jax.nn.gelu(
        jnp.dot(
            features.reshape(seq_dev * images, width), critic_in, preferred_element_type=jnp.float32
        ),
        approximate=True,
    )
    logits = jnp.dot(
        critic_hidden,
        critic_out,
        precision=lax.Precision.HIGHEST,
        preferred_element_type=jnp.float32,
    )
    return features, logits.reshape(seq_dev, images)


def solution(mesh):
    return jax.shard_map(
        local,
        mesh=mesh,
        in_specs=(
            P("rep", "expert", None, None),
            P("rep", "expert", None, None),
            P("rep", "expert", None, None),
            P(),
            P("expert", None, "rep"),
            P("expert", None, "rep"),
            P("expert", "rep", None),
            P(),
            P(None, None, "rep", None),
            P(None, "rep", None),
            P("rep", None, None),
            P(),
            P(),
        ),
        out_specs=(P("rep", "expert", None, None), P("rep", "expert", None)),
        check_vma=False,
    )
```

```python
import functools

import jax
import jax.numpy as jnp
from jax import lax
from jax.experimental import pallas as pl
from jax.sharding import PartitionSpec as P


def norm_rows(values, gain):
    return values * lax.rsqrt(jnp.mean(values * values, axis=-1, keepdims=True) + 1e-06) * gain


def slot_numbers(chosen, count):
    onehot = (chosen[..., None] == jnp.arange(count, dtype=jnp.int32)).astype(jnp.int32)
    before = jnp.cumsum(onehot, axis=-2) - onehot
    return jnp.sum(before * onehot, axis=-1)


def attention_kernel(query_ref, key_ref, value_ref, out_ref, *, scale):
    scores = lax.dot_general(
        query_ref[...],
        key_ref[...],
        (((1,), (1,)), ((), ())),
        preferred_element_type=jnp.float32,
    ) * scale
    scores = scores - jnp.max(scores, axis=-1, keepdims=True)
    weights = jnp.exp(scores)
    probs = (weights / jnp.sum(weights, axis=-1, keepdims=True)).astype(jnp.bfloat16)
    out_ref[...] = jnp.dot(probs, value_ref[...], preferred_element_type=jnp.float32).astype(
        out_ref.dtype
    )


def attention(whole, scale, interpret=False):
    _, pairs, seq_len, head_size = whole.shape
    block = min(256, seq_len)
    return pl.pallas_call(
        functools.partial(attention_kernel, scale=scale),
        grid=(pairs, seq_len // block),
        in_specs=[
            pl.BlockSpec((None, None, block, head_size), lambda p, i: (0, p, i, 0)),
            pl.BlockSpec((None, None, seq_len, head_size), lambda p, i: (1, p, 0, 0)),
            pl.BlockSpec((None, None, seq_len, head_size), lambda p, i: (2, p, 0, 0)),
        ],
        out_specs=pl.BlockSpec((None, block, head_size), lambda p, i: (p, i, 0)),
        out_shape=jax.ShapeDtypeStruct((pairs, seq_len, head_size), whole.dtype),
        interpret=interpret,
    )(whole, whole, whole)


def gather_rep(values, axis, count):
    if count % 2 != 0 or count < 4:
        return lax.all_gather(values, "rep", axis=axis, tiled=True)
    half = count // 2
    across = [[i, i + half] for i in range(half)]
    within = [[2 * i, 2 * i + 1] for i in range(half)] if half == 2 else None
    if within is None:
        return lax.all_gather(values, "rep", axis=axis, tiled=True)
    first = lax.all_gather(values, "rep", axis=axis, tiled=True, axis_index_groups=across)
    return lax.all_gather(first, "rep", axis=axis, tiled=True, axis_index_groups=within)


def local(
    tokens,
    expert_ids,
    gate_probs,
    norm_gain,
    expert_gate,
    expert_up,
    expert_down,
    teacher_gain,
    teacher_qkv,
    qk_gain,
    teacher_out,
    critic_in,
    critic_out,
):
    seq_dev = tokens.shape[1]
    images = tokens.shape[2]
    width = tokens.shape[3]
    tok_count = seq_dev * images
    n_owner = lax.axis_size("expert")
    n_replica = lax.axis_size("rep")
    exp_local = expert_gate.shape[0]
    expert_total = exp_local * n_owner
    capacity = max(2, tok_count * 10 // (4 * expert_total))
    gate_full = gather_rep(expert_gate, 2, n_replica)
    up_full = gather_rep(expert_up, 2, n_replica)
    down_full = gather_rep(expert_down, 1, n_replica)
    qkv_full = lax.all_gather(teacher_qkv, "rep", axis=2, tiled=True)
    qk_gain_full = lax.all_gather(qk_gain, "rep", axis=1, tiled=True)
    out_full = lax.all_gather(teacher_out, "rep", axis=0, tiled=True)
    residual = tokens.reshape(tok_count, width).astype(jnp.float32)
    normed = norm_rows(residual, norm_gain).astype(jnp.bfloat16)
    chosen = expert_ids.reshape(2 * tok_count)
    slot_index = slot_numbers(chosen, expert_total)
    gate_value = gate_probs.reshape(2 * tok_count)
    target = chosen * capacity + slot_index
    rows_all = jnp.arange(expert_total * capacity, dtype=jnp.int32)
    assign_rows = (target[:, None] == rows_all[None, :]).astype(jnp.bfloat16)
    token_rows = assign_rows.reshape(tok_count, 2, expert_total * capacity).sum(axis=1)
    outgoing = jnp.einsum(
        "tr,td->rd", token_rows, normed, preferred_element_type=jnp.float32
    ).astype(jnp.bfloat16)
    outgoing = outgoing.reshape(n_owner, exp_local * capacity, width)
    arrived = lax.all_to_all(outgoing, "expert", split_axis=0, concat_axis=0, tiled=True)
    arrived = arrived.reshape(n_owner, exp_local, capacity, width)
    gate_part = jnp.einsum(
        "sjcd,jdf->sjcf", arrived, gate_full, preferred_element_type=jnp.float32
    )
    up_part = jnp.einsum("sjcd,jdf->sjcf", arrived, up_full, preferred_element_type=jnp.float32)
    hidden = (jax.nn.silu(gate_part) * up_part).astype(jnp.bfloat16)
    ff_total = hidden.shape[-1]
    ff_part = ff_total // n_replica
    produced = jnp.zeros(arrived.shape, jnp.float32)
    for part in range(n_replica):
        low = part * ff_part
        produced = produced + jnp.einsum(
            "sjcf,jfd->sjcd",
            hidden[..., low:low + ff_part],
            down_full[:, low:low + ff_part],
            preferred_element_type=jnp.float32,
        ).astype(jnp.bfloat16).astype(jnp.float32)
    results = produced.astype(jnp.bfloat16).reshape(n_owner, exp_local * capacity, width)
    returned = lax.all_to_all(results, "expert", split_axis=0, concat_axis=0, tiled=True).reshape(
        expert_total * capacity, width
    )
    picked = jnp.einsum(
        "tkr,rd->ktd",
        assign_rows.reshape(tok_count, 2, expert_total * capacity),
        returned,
        preferred_element_type=jnp.float32,
    )
    gate_pair = gate_value.reshape(tok_count, 2)
    combined = picked[0] * gate_pair[:, 0:1] + picked[1] * gate_pair[:, 1:2]
    mixed = (residual + combined).astype(jnp.bfloat16)
    teacher_in = norm_rows(mixed.astype(jnp.float32), teacher_gain).astype(jnp.bfloat16)
    teacher_in = teacher_in.reshape(seq_dev, images, width)
    mixed = mixed.reshape(seq_dev, images, width)
    heads_all = qkv_full.shape[2]
    head_size = qkv_full.shape[3]
    chunks = images if (heads_all % n_owner == 0) else 1
    per_chunk = images // chunks
    features_parts = []
    logits_parts = []
    for chunk in range(chunks):
        sel = slice(chunk * per_chunk, (chunk + 1) * per_chunk)
        features, logits = teach(
            teacher_in[:, sel], mixed[:, sel], qkv_full, qk_gain_full, out_full, critic_in, critic_out,
            n_replica,
        )
        features_parts.append(features)
        logits_parts.append(logits)
    features = jnp.concatenate(features_parts, axis=1)
    logits = jnp.concatenate(logits_parts, axis=1)
    return (features.reshape(1, seq_dev, images, width), logits.reshape(1, seq_dev, images))


def teach(teacher_in, mixed, qkv_full, qk_gain_full, out_full, critic_in, critic_out, n_replica):
    seq_dev, images, width = teacher_in.shape
    heads_all = qkv_full.shape[2]
    head_size = qkv_full.shape[3]
    projected = jnp.einsum(
        "sid,djhe->jihse", teacher_in, qkv_full, preferred_element_type=jnp.float32
    )
    query = norm_rows(projected[0], qk_gain_full[0][:, None, :])
    keyed = norm_rows(projected[1], qk_gain_full[1][:, None, :])
    projected = jnp.stack([query, keyed, projected[2]]).astype(jnp.bfloat16)
    pairs_all = images * heads_all
    grouped = projected.reshape(3, pairs_all, seq_dev, head_size)
    whole = lax.all_to_all(grouped, "expert", split_axis=1, concat_axis=2, tiled=True)
    attended = attention(whole, head_size ** (-0.5))
    gathered_heads = lax.all_to_all(attended, "expert", split_axis=1, concat_axis=0, tiled=True)
    gathered_heads = gathered_heads.reshape(images, heads_all, seq_dev, head_size)
    heads_part = heads_all // n_replica
    projected_out = jnp.zeros((seq_dev, images, width), jnp.float32)
    for part in range(n_replica):
        low = part * heads_part
        projected_out = projected_out + jnp.einsum(
            "ihse,hed->sid",
            gathered_heads[:, low:low + heads_part],
            out_full[low:low + heads_part],
            preferred_element_type=jnp.float32,
        ).astype(jnp.bfloat16).astype(jnp.float32)
    features = (mixed.astype(jnp.float32) + projected_out).astype(jnp.bfloat16)
    critic_hidden = jax.nn.gelu(
        jnp.dot(
            features.reshape(seq_dev * images, width), critic_in, preferred_element_type=jnp.float32
        ),
        approximate=True,
    )
    logits = jnp.dot(
        critic_hidden,
        critic_out,
        precision=lax.Precision.HIGHEST,
        preferred_element_type=jnp.float32,
    )
    return features, logits.reshape(seq_dev, images)


def solution(mesh):
    return jax.shard_map(
        local,
        mesh=mesh,
        in_specs=(
            P("rep", "expert", None, None),
            P("rep", "expert", None, None),
            P("rep", "expert", None, None),
            P(),
            P("expert", None, "rep"),
            P("expert", None, "rep"),
            P("expert", "rep", None),
            P(),
            P(None, None, "rep", None),
            P(None, "rep", None),
            P("rep", None, None),
            P(),
            P(),
        ),
        out_specs=(P("rep", "expert", None, None), P("rep", "expert", None)),
        check_vma=False,
    )
```

```python
import functools

import jax
import jax.numpy as jnp
from jax import lax
from jax.experimental import pallas as pl
from jax.sharding import PartitionSpec as P


def norm_rows(values, gain):
    return values * lax.rsqrt(jnp.mean(values * values, axis=-1, keepdims=True) + 1e-06) * gain


def slot_numbers(chosen, count):
    onehot = (chosen[..., None] == jnp.arange(count, dtype=jnp.int32)).astype(jnp.int32)
    before = jnp.cumsum(onehot, axis=-2) - onehot
    return jnp.sum(before * onehot, axis=-1)


def attention_kernel(query_ref, key_ref, value_ref, out_ref, *, scale):
    scores = lax.dot_general(
        query_ref[...],
        key_ref[...],
        (((1,), (1,)), ((), ())),
        preferred_element_type=jnp.float32,
    ) * scale
    scores = scores - jnp.max(scores, axis=-1, keepdims=True)
    weights = jnp.exp(scores)
    probs = (weights / jnp.sum(weights, axis=-1, keepdims=True)).astype(jnp.bfloat16)
    out_ref[...] = jnp.dot(probs, value_ref[...], preferred_element_type=jnp.float32).astype(
        out_ref.dtype
    )


def attention(whole, scale, interpret=False):
    _, pairs, seq_len, head_size = whole.shape
    block = min(256, seq_len)
    return pl.pallas_call(
        functools.partial(attention_kernel, scale=scale),
        grid=(pairs, seq_len // block),
        in_specs=[
            pl.BlockSpec((None, None, block, head_size), lambda p, i: (0, p, i, 0)),
            pl.BlockSpec((None, None, seq_len, head_size), lambda p, i: (1, p, 0, 0)),
            pl.BlockSpec((None, None, seq_len, head_size), lambda p, i: (2, p, 0, 0)),
        ],
        out_specs=pl.BlockSpec((None, block, head_size), lambda p, i: (p, i, 0)),
        out_shape=jax.ShapeDtypeStruct((pairs, seq_len, head_size), whole.dtype),
        interpret=interpret,
    )(whole, whole, whole)


def local(
    tokens,
    expert_ids,
    gate_probs,
    norm_gain,
    expert_gate,
    expert_up,
    expert_down,
    teacher_gain,
    teacher_qkv,
    qk_gain,
    teacher_out,
    critic_in,
    critic_out,
):
    seq_dev = tokens.shape[1]
    images = tokens.shape[2]
    width = tokens.shape[3]
    tok_count = seq_dev * images
    n_owner = lax.axis_size("expert")
    n_replica = lax.axis_size("rep")
    exp_local = expert_gate.shape[0]
    expert_total = exp_local * n_owner
    capacity = max(2, tok_count * 10 // (4 * expert_total))
    gate_full = lax.all_gather(expert_gate, "rep", axis=2, tiled=True)
    up_full = lax.all_gather(expert_up, "rep", axis=2, tiled=True)
    down_full = lax.all_gather(expert_down, "rep", axis=1, tiled=True)
    qkv_full = lax.all_gather(teacher_qkv, "rep", axis=2, tiled=True)
    qk_gain_full = lax.all_gather(qk_gain, "rep", axis=1, tiled=True)
    out_full = lax.all_gather(teacher_out, "rep", axis=0, tiled=True)
    residual = tokens.reshape(tok_count, width).astype(jnp.float32)
    normed = norm_rows(residual, norm_gain).astype(jnp.bfloat16)
    chosen = expert_ids.reshape(2 * tok_count)
    slot_index = slot_numbers(chosen, expert_total)
    gate_value = gate_probs.reshape(2 * tok_count)
    target = chosen * capacity + slot_index
    rows_all = jnp.arange(expert_total * capacity, dtype=jnp.int32)
    target_pair = target.reshape(tok_count, 2)
    first_rows = (target_pair[:, 0:1] == rows_all[None, :]).astype(jnp.bfloat16)
    second_rows = (target_pair[:, 1:2] == rows_all[None, :]).astype(jnp.bfloat16)
    token_rows = first_rows + second_rows
    outgoing = jnp.einsum(
        "tr,td->rd", token_rows, normed, preferred_element_type=jnp.float32
    ).astype(jnp.bfloat16)
    outgoing = outgoing.reshape(n_owner, exp_local * capacity, width)
    arrived = lax.all_to_all(outgoing, "expert", split_axis=0, concat_axis=0, tiled=True)
    arrived = arrived.reshape(n_owner, exp_local, capacity, width)
    gate_part = jnp.einsum(
        "sjcd,jdf->sjcf", arrived, gate_full, preferred_element_type=jnp.float32
    )
    up_part = jnp.einsum("sjcd,jdf->sjcf", arrived, up_full, preferred_element_type=jnp.float32)
    hidden = (jax.nn.silu(gate_part) * up_part).astype(jnp.bfloat16)
    ff_total = hidden.shape[-1]
    ff_part = ff_total // n_replica
    produced = jnp.zeros(arrived.shape, jnp.float32)
    for part in range(n_replica):
        low = part * ff_part
        produced = produced + jnp.einsum(
            "sjcf,jfd->sjcd",
            hidden[..., low:low + ff_part],
            down_full[:, low:low + ff_part],
            preferred_element_type=jnp.float32,
        ).astype(jnp.bfloat16).astype(jnp.float32)
    results = produced.astype(jnp.bfloat16).reshape(n_owner, exp_local * capacity, width)
    returned = lax.all_to_all(results, "expert", split_axis=0, concat_axis=0, tiled=True).reshape(
        expert_total * capacity, width
    )
    gate_pair = gate_value.reshape(tok_count, 2)
    combined = jnp.dot(first_rows, returned, preferred_element_type=jnp.float32) * gate_pair[
        :, 0:1
    ] + jnp.dot(second_rows, returned, preferred_element_type=jnp.float32) * gate_pair[:, 1:2]
    mixed = (residual + combined).astype(jnp.bfloat16)
    teacher_in = norm_rows(mixed.astype(jnp.float32), teacher_gain).astype(jnp.bfloat16)
    teacher_in = teacher_in.reshape(seq_dev, images, width)
    mixed = mixed.reshape(seq_dev, images, width)
    heads_all = qkv_full.shape[2]
    head_size = qkv_full.shape[3]
    chunks = images if (heads_all % n_owner == 0) else 1
    per_chunk = images // chunks
    features_parts = []
    logits_parts = []
    for chunk in range(chunks):
        sel = slice(chunk * per_chunk, (chunk + 1) * per_chunk)
        features, logits = teach(
            teacher_in[:, sel], mixed[:, sel], qkv_full, qk_gain_full, out_full, critic_in, critic_out,
            n_replica,
        )
        features_parts.append(features)
        logits_parts.append(logits)
    features = jnp.concatenate(features_parts, axis=1)
    logits = jnp.concatenate(logits_parts, axis=1)
    return (features.reshape(1, seq_dev, images, width), logits.reshape(1, seq_dev, images))


def teach(teacher_in, mixed, qkv_full, qk_gain_full, out_full, critic_in, critic_out, n_replica):
    seq_dev, images, width = teacher_in.shape
    heads_all = qkv_full.shape[2]
    head_size = qkv_full.shape[3]
    projected = jnp.einsum(
        "sid,djhe->jihse", teacher_in, qkv_full, preferred_element_type=jnp.float32
    )
    query = norm_rows(projected[0], qk_gain_full[0][:, None, :])
    keyed = norm_rows(projected[1], qk_gain_full[1][:, None, :])
    projected = jnp.stack([query, keyed, projected[2]]).astype(jnp.bfloat16)
    pairs_all = images * heads_all
    grouped = projected.reshape(3, pairs_all, seq_dev, head_size)
    whole = lax.all_to_all(grouped, "expert", split_axis=1, concat_axis=2, tiled=True)
    attended = attention(whole, head_size ** (-0.5))
    gathered_heads = lax.all_to_all(attended, "expert", split_axis=1, concat_axis=0, tiled=True)
    gathered_heads = gathered_heads.reshape(images, heads_all, seq_dev, head_size)
    heads_part = heads_all // n_replica
    projected_out = jnp.zeros((seq_dev, images, width), jnp.float32)
    for part in range(n_replica):
        low = part * heads_part
        projected_out = projected_out + jnp.einsum(
            "ihse,hed->sid",
            gathered_heads[:, low:low + heads_part],
            out_full[low:low + heads_part],
            preferred_element_type=jnp.float32,
        ).astype(jnp.bfloat16).astype(jnp.float32)
    features = (mixed.astype(jnp.float32) + projected_out).astype(jnp.bfloat16)
    critic_hidden = jax.nn.gelu(
        jnp.dot(
            features.reshape(seq_dev * images, width), critic_in, preferred_element_type=jnp.float32
        ),
        approximate=True,
    )
    logits = jnp.dot(
        critic_hidden,
        critic_out,
        precision=lax.Precision.HIGHEST,
        preferred_element_type=jnp.float32,
    )
    return features, logits.reshape(seq_dev, images)


def solution(mesh):
    return jax.shard_map(
        local,
        mesh=mesh,
        in_specs=(
            P("rep", "expert", None, None),
            P("rep", "expert", None, None),
            P("rep", "expert", None, None),
            P(),
            P("expert", None, "rep"),
            P("expert", None, "rep"),
            P("expert", "rep", None),
            P(),
            P(None, None, "rep", None),
            P(None, "rep", None),
            P("rep", None, None),
            P(),
            P(),
        ),
        out_specs=(P("rep", "expert", None, None), P("rep", "expert", None)),
        check_vma=False,
    )
```

```python
import functools

import jax
import jax.numpy as jnp
from jax import lax
from jax.experimental import pallas as pl
from jax.sharding import PartitionSpec as P


def norm_rows(values, gain):
    return values * lax.rsqrt(jnp.mean(values * values, axis=-1, keepdims=True) + 1e-06) * gain


def slot_numbers(chosen, count):
    onehot = (chosen[..., None] == jnp.arange(count, dtype=jnp.int32)).astype(jnp.int32)
    before = jnp.cumsum(onehot, axis=-2) - onehot
    return jnp.sum(before * onehot, axis=-1)


def attention_kernel(query_ref, key_ref, value_ref, out_ref, *, scale):
    scores = lax.dot_general(
        query_ref[...],
        key_ref[...],
        (((1,), (1,)), ((), ())),
        preferred_element_type=jnp.float32,
    ) * scale
    scores = scores - jnp.max(scores, axis=-1, keepdims=True)
    weights = jnp.exp(scores)
    probs = (weights / jnp.sum(weights, axis=-1, keepdims=True)).astype(jnp.bfloat16)
    out_ref[...] = jnp.dot(probs, value_ref[...], preferred_element_type=jnp.float32).astype(
        out_ref.dtype
    )


def attention(whole, scale, interpret=False):
    _, pairs, seq_len, head_size = whole.shape
    block = min(256, seq_len)
    return pl.pallas_call(
        functools.partial(attention_kernel, scale=scale),
        grid=(pairs, seq_len // block),
        in_specs=[
            pl.BlockSpec((None, None, block, head_size), lambda p, i: (0, p, i, 0)),
            pl.BlockSpec((None, None, seq_len, head_size), lambda p, i: (1, p, 0, 0)),
            pl.BlockSpec((None, None, seq_len, head_size), lambda p, i: (2, p, 0, 0)),
        ],
        out_specs=pl.BlockSpec((None, block, head_size), lambda p, i: (p, i, 0)),
        out_shape=jax.ShapeDtypeStruct((pairs, seq_len, head_size), whole.dtype),
        interpret=interpret,
    )(whole, whole, whole)


def local(
    tokens,
    expert_ids,
    gate_probs,
    norm_gain,
    expert_gate,
    expert_up,
    expert_down,
    teacher_gain,
    teacher_qkv,
    qk_gain,
    teacher_out,
    critic_in,
    critic_out,
):
    seq_dev = tokens.shape[1]
    images = tokens.shape[2]
    width = tokens.shape[3]
    tok_count = seq_dev * images
    n_owner = lax.axis_size("expert")
    n_replica = lax.axis_size("rep")
    exp_local = expert_gate.shape[0]
    expert_total = exp_local * n_owner
    capacity = max(2, tok_count * 10 // (4 * expert_total))
    expert_weights = [
        (
            lax.all_gather(expert_gate[j], "rep", axis=1, tiled=True),
            lax.all_gather(expert_up[j], "rep", axis=1, tiled=True),
            lax.all_gather(expert_down[j], "rep", axis=0, tiled=True),
        )
        for j in range(exp_local)
    ]
    qkv_full = lax.all_gather(teacher_qkv, "rep", axis=2, tiled=True)
    qk_gain_full = lax.all_gather(qk_gain, "rep", axis=1, tiled=True)
    out_full = lax.all_gather(teacher_out, "rep", axis=0, tiled=True)
    residual = tokens.reshape(tok_count, width).astype(jnp.float32)
    normed = norm_rows(residual, norm_gain).astype(jnp.bfloat16)
    chosen = expert_ids.reshape(2 * tok_count)
    slot_index = slot_numbers(chosen, expert_total)
    gate_value = gate_probs.reshape(2 * tok_count)
    target = chosen * capacity + slot_index
    rows_all = jnp.arange(expert_total * capacity, dtype=jnp.int32)
    target_pair = target.reshape(tok_count, 2)
    first_rows = (target_pair[:, 0:1] == rows_all[None, :]).astype(jnp.bfloat16)
    second_rows = (target_pair[:, 1:2] == rows_all[None, :]).astype(jnp.bfloat16)
    token_rows = first_rows + second_rows
    outgoing = jnp.einsum(
        "tr,td->rd", token_rows, normed, preferred_element_type=jnp.float32
    ).astype(jnp.bfloat16)
    outgoing = outgoing.reshape(n_owner, exp_local * capacity, width)
    arrived = lax.all_to_all(outgoing, "expert", split_axis=0, concat_axis=0, tiled=True)
    arrived = arrived.reshape(n_owner, exp_local, capacity, width)
    returned_parts = []
    for j, (gate_w, up_w, down_w) in enumerate(expert_weights):
        rows = arrived[:, j]
        gate_part = jnp.einsum("scd,df->scf", rows, gate_w, preferred_element_type=jnp.float32)
        up_part = jnp.einsum("scd,df->scf", rows, up_w, preferred_element_type=jnp.float32)
        hidden = (jax.nn.silu(gate_part) * up_part).astype(jnp.bfloat16)
        ff_total = hidden.shape[-1]
        ff_part = ff_total // n_replica
        produced = jnp.zeros(rows.shape, jnp.float32)
        for part in range(n_replica):
            low = part * ff_part
            produced = produced + jnp.einsum(
                "scf,fd->scd",
                hidden[..., low:low + ff_part],
                down_w[low:low + ff_part],
                preferred_element_type=jnp.float32,
            ).astype(jnp.bfloat16).astype(jnp.float32)
        returned_parts.append(
            lax.all_to_all(
                produced.astype(jnp.bfloat16), "expert", split_axis=0, concat_axis=0, tiled=True
            )
        )
    returned = jnp.stack(returned_parts, axis=1).reshape(expert_total * capacity, width)
    gate_pair = gate_value.reshape(tok_count, 2)
    combined = jnp.dot(first_rows, returned, preferred_element_type=jnp.float32) * gate_pair[
        :, 0:1
    ] + jnp.dot(second_rows, returned, preferred_element_type=jnp.float32) * gate_pair[:, 1:2]
    mixed = (residual + combined).astype(jnp.bfloat16)
    teacher_in = norm_rows(mixed.astype(jnp.float32), teacher_gain).astype(jnp.bfloat16)
    teacher_in = teacher_in.reshape(seq_dev, images, width)
    mixed = mixed.reshape(seq_dev, images, width)
    heads_all = qkv_full.shape[2]
    head_size = qkv_full.shape[3]
    chunks = images if (heads_all % n_owner == 0) else 1
    per_chunk = images // chunks
    features_parts = []
    logits_parts = []
    for chunk in range(chunks):
        sel = slice(chunk * per_chunk, (chunk + 1) * per_chunk)
        features, logits = teach(
            teacher_in[:, sel], mixed[:, sel], qkv_full, qk_gain_full, out_full, critic_in, critic_out,
            n_replica,
        )
        features_parts.append(features)
        logits_parts.append(logits)
    features = jnp.concatenate(features_parts, axis=1)
    logits = jnp.concatenate(logits_parts, axis=1)
    return (features.reshape(1, seq_dev, images, width), logits.reshape(1, seq_dev, images))


def teach(teacher_in, mixed, qkv_full, qk_gain_full, out_full, critic_in, critic_out, n_replica):
    seq_dev, images, width = teacher_in.shape
    heads_all = qkv_full.shape[2]
    head_size = qkv_full.shape[3]
    projected = jnp.einsum(
        "sid,djhe->jihse", teacher_in, qkv_full, preferred_element_type=jnp.float32
    )
    query = norm_rows(projected[0], qk_gain_full[0][:, None, :])
    keyed = norm_rows(projected[1], qk_gain_full[1][:, None, :])
    projected = jnp.stack([query, keyed, projected[2]]).astype(jnp.bfloat16)
    pairs_all = images * heads_all
    grouped = projected.reshape(3, pairs_all, seq_dev, head_size)
    whole = lax.all_to_all(grouped, "expert", split_axis=1, concat_axis=2, tiled=True)
    attended = attention(whole, head_size ** (-0.5))
    gathered_heads = lax.all_to_all(attended, "expert", split_axis=1, concat_axis=0, tiled=True)
    gathered_heads = gathered_heads.reshape(images, heads_all, seq_dev, head_size)
    heads_part = heads_all // n_replica
    projected_out = jnp.zeros((seq_dev, images, width), jnp.float32)
    for part in range(n_replica):
        low = part * heads_part
        projected_out = projected_out + jnp.einsum(
            "ihse,hed->sid",
            gathered_heads[:, low:low + heads_part],
            out_full[low:low + heads_part],
            preferred_element_type=jnp.float32,
        ).astype(jnp.bfloat16).astype(jnp.float32)
    features = (mixed.astype(jnp.float32) + projected_out).astype(jnp.bfloat16)
    critic_hidden = jax.nn.gelu(
        jnp.dot(
            features.reshape(seq_dev * images, width), critic_in, preferred_element_type=jnp.float32
        ),
        approximate=True,
    )
    logits = jnp.dot(
        critic_hidden,
        critic_out,
        precision=lax.Precision.HIGHEST,
        preferred_element_type=jnp.float32,
    )
    return features, logits.reshape(seq_dev, images)


def solution(mesh):
    return jax.shard_map(
        local,
        mesh=mesh,
        in_specs=(
            P("rep", "expert", None, None),
            P("rep", "expert", None, None),
            P("rep", "expert", None, None),
            P(),
            P("expert", None, "rep"),
            P("expert", None, "rep"),
            P("expert", "rep", None),
            P(),
            P(None, None, "rep", None),
            P(None, "rep", None),
            P("rep", None, None),
            P(),
            P(),
        ),
        out_specs=(P("rep", "expert", None, None), P("rep", "expert", None)),
        check_vma=False,
    )
```

```python
import functools

import jax
import jax.numpy as jnp
from jax import lax
from jax.experimental import pallas as pl
from jax.sharding import PartitionSpec as P


def norm_rows(values, gain):
    return values * lax.rsqrt(jnp.mean(values * values, axis=-1, keepdims=True) + 1e-06) * gain


def slot_numbers(chosen, count):
    onehot = (chosen[..., None] == jnp.arange(count, dtype=jnp.int32)).astype(jnp.int32)
    before = jnp.cumsum(onehot, axis=-2) - onehot
    return jnp.sum(before * onehot, axis=-1)


def attention_kernel(query_ref, key_ref, value_ref, out_ref, *, scale):
    scores = lax.dot_general(
        query_ref[...],
        key_ref[...],
        (((1,), (1,)), ((), ())),
        preferred_element_type=jnp.float32,
    ) * scale
    scores = scores - jnp.max(scores, axis=-1, keepdims=True)
    weights = jnp.exp(scores)
    probs = (weights / jnp.sum(weights, axis=-1, keepdims=True)).astype(jnp.bfloat16)
    out_ref[...] = jnp.dot(probs, value_ref[...], preferred_element_type=jnp.float32).astype(
        out_ref.dtype
    )


def attention(whole, scale, interpret=False):
    _, pairs, seq_len, head_size = whole.shape
    block = min(256, seq_len)
    return pl.pallas_call(
        functools.partial(attention_kernel, scale=scale),
        grid=(pairs, seq_len // block),
        in_specs=[
            pl.BlockSpec((None, None, block, head_size), lambda p, i: (0, p, i, 0)),
            pl.BlockSpec((None, None, seq_len, head_size), lambda p, i: (1, p, 0, 0)),
            pl.BlockSpec((None, None, seq_len, head_size), lambda p, i: (2, p, 0, 0)),
        ],
        out_specs=pl.BlockSpec((None, block, head_size), lambda p, i: (p, i, 0)),
        out_shape=jax.ShapeDtypeStruct((pairs, seq_len, head_size), whole.dtype),
        interpret=interpret,
    )(whole, whole, whole)


def local(
    tokens,
    expert_ids,
    gate_probs,
    norm_gain,
    expert_gate,
    expert_up,
    expert_down,
    teacher_gain,
    teacher_qkv,
    qk_gain,
    teacher_out,
    critic_in,
    critic_out,
):
    seq_dev = tokens.shape[1]
    images = tokens.shape[2]
    width = tokens.shape[3]
    tok_count = seq_dev * images
    n_owner = lax.axis_size("expert")
    n_replica = lax.axis_size("rep")
    exp_local = expert_gate.shape[0]
    expert_total = exp_local * n_owner
    capacity = max(2, tok_count * 10 // (4 * expert_total))
    gate_full = lax.all_gather(expert_gate, "rep", axis=2, tiled=True)
    up_full = lax.all_gather(expert_up, "rep", axis=2, tiled=True)
    down_parts = [
        lax.all_gather(expert_down[j], "rep", axis=0, tiled=True) for j in range(exp_local)
    ]
    qkv_full = lax.all_gather(teacher_qkv, "rep", axis=2, tiled=True)
    qk_gain_full = lax.all_gather(qk_gain, "rep", axis=1, tiled=True)
    out_full = lax.all_gather(teacher_out, "rep", axis=0, tiled=True)
    residual = tokens.reshape(tok_count, width).astype(jnp.float32)
    normed = norm_rows(residual, norm_gain).astype(jnp.bfloat16)
    chosen = expert_ids.reshape(2 * tok_count)
    slot_index = slot_numbers(chosen, expert_total)
    gate_value = gate_probs.reshape(2 * tok_count)
    target = chosen * capacity + slot_index
    rows_all = jnp.arange(expert_total * capacity, dtype=jnp.int32)
    target_pair = target.reshape(tok_count, 2)
    first_rows = (target_pair[:, 0:1] == rows_all[None, :]).astype(jnp.bfloat16)
    second_rows = (target_pair[:, 1:2] == rows_all[None, :]).astype(jnp.bfloat16)
    token_rows = first_rows + second_rows
    outgoing = jnp.einsum(
        "tr,td->rd", token_rows, normed, preferred_element_type=jnp.float32
    ).astype(jnp.bfloat16)
    outgoing = outgoing.reshape(n_owner, exp_local * capacity, width)
    arrived = lax.all_to_all(outgoing, "expert", split_axis=0, concat_axis=0, tiled=True)
    arrived = arrived.reshape(n_owner, exp_local, capacity, width)
    gate_part = jnp.einsum(
        "sjcd,jdf->sjcf", arrived, gate_full, preferred_element_type=jnp.float32
    )
    up_part = jnp.einsum("sjcd,jdf->sjcf", arrived, up_full, preferred_element_type=jnp.float32)
    hidden = (jax.nn.silu(gate_part) * up_part).astype(jnp.bfloat16)
    ff_total = hidden.shape[-1]
    ff_part = ff_total // n_replica
    returned_parts = []
    for j, down_w in enumerate(down_parts):
        produced = jnp.zeros(arrived[:, j].shape, jnp.float32)
        for part in range(n_replica):
            low = part * ff_part
            produced = produced + jnp.einsum(
                "scf,fd->scd",
                hidden[:, j, :, low:low + ff_part],
                down_w[low:low + ff_part],
                preferred_element_type=jnp.float32,
            ).astype(jnp.bfloat16).astype(jnp.float32)
        returned_parts.append(
            lax.all_to_all(
                produced.astype(jnp.bfloat16), "expert", split_axis=0, concat_axis=0, tiled=True
            )
        )
    returned = jnp.stack(returned_parts, axis=1).reshape(expert_total * capacity, width)
    gate_pair = gate_value.reshape(tok_count, 2)
    combined = jnp.dot(first_rows, returned, preferred_element_type=jnp.float32) * gate_pair[
        :, 0:1
    ] + jnp.dot(second_rows, returned, preferred_element_type=jnp.float32) * gate_pair[:, 1:2]
    mixed = (residual + combined).astype(jnp.bfloat16)
    teacher_in = norm_rows(mixed.astype(jnp.float32), teacher_gain).astype(jnp.bfloat16)
    teacher_in = teacher_in.reshape(seq_dev, images, width)
    mixed = mixed.reshape(seq_dev, images, width)
    heads_all = qkv_full.shape[2]
    head_size = qkv_full.shape[3]
    chunks = images if (heads_all % n_owner == 0) else 1
    per_chunk = images // chunks
    features_parts = []
    logits_parts = []
    for chunk in range(chunks):
        sel = slice(chunk * per_chunk, (chunk + 1) * per_chunk)
        features, logits = teach(
            teacher_in[:, sel], mixed[:, sel], qkv_full, qk_gain_full, out_full, critic_in, critic_out,
            n_replica,
        )
        features_parts.append(features)
        logits_parts.append(logits)
    features = jnp.concatenate(features_parts, axis=1)
    logits = jnp.concatenate(logits_parts, axis=1)
    return (features.reshape(1, seq_dev, images, width), logits.reshape(1, seq_dev, images))


def teach(teacher_in, mixed, qkv_full, qk_gain_full, out_full, critic_in, critic_out, n_replica):
    seq_dev, images, width = teacher_in.shape
    heads_all = qkv_full.shape[2]
    head_size = qkv_full.shape[3]
    projected = jnp.einsum(
        "sid,djhe->jihse", teacher_in, qkv_full, preferred_element_type=jnp.float32
    )
    query = norm_rows(projected[0], qk_gain_full[0][:, None, :])
    keyed = norm_rows(projected[1], qk_gain_full[1][:, None, :])
    projected = jnp.stack([query, keyed, projected[2]]).astype(jnp.bfloat16)
    pairs_all = images * heads_all
    grouped = projected.reshape(3, pairs_all, seq_dev, head_size)
    whole = lax.all_to_all(grouped, "expert", split_axis=1, concat_axis=2, tiled=True)
    attended = attention(whole, head_size ** (-0.5))
    gathered_heads = lax.all_to_all(attended, "expert", split_axis=1, concat_axis=0, tiled=True)
    gathered_heads = gathered_heads.reshape(images, heads_all, seq_dev, head_size)
    heads_part = heads_all // n_replica
    projected_out = jnp.zeros((seq_dev, images, width), jnp.float32)
    for part in range(n_replica):
        low = part * heads_part
        projected_out = projected_out + jnp.einsum(
            "ihse,hed->sid",
            gathered_heads[:, low:low + heads_part],
            out_full[low:low + heads_part],
            preferred_element_type=jnp.float32,
        ).astype(jnp.bfloat16).astype(jnp.float32)
    features = (mixed.astype(jnp.float32) + projected_out).astype(jnp.bfloat16)
    critic_hidden = jax.nn.gelu(
        jnp.dot(
            features.reshape(seq_dev * images, width), critic_in, preferred_element_type=jnp.float32
        ),
        approximate=True,
    )
    logits = jnp.dot(
        critic_hidden,
        critic_out,
        precision=lax.Precision.HIGHEST,
        preferred_element_type=jnp.float32,
    )
    return features, logits.reshape(seq_dev, images)


def solution(mesh):
    return jax.shard_map(
        local,
        mesh=mesh,
        in_specs=(
            P("rep", "expert", None, None),
            P("rep", "expert", None, None),
            P("rep", "expert", None, None),
            P(),
            P("expert", None, "rep"),
            P("expert", None, "rep"),
            P("expert", "rep", None),
            P(),
            P(None, None, "rep", None),
            P(None, "rep", None),
            P("rep", None, None),
            P(),
            P(),
        ),
        out_specs=(P("rep", "expert", None, None), P("rep", "expert", None)),
        check_vma=False,
    )
```

```python
import functools

import jax
import jax.numpy as jnp
from jax import lax
from jax.experimental import pallas as pl
from jax.sharding import PartitionSpec as P


def norm_rows(values, gain):
    return values * lax.rsqrt(jnp.mean(values * values, axis=-1, keepdims=True) + 1e-06) * gain


def slot_numbers(chosen, count):
    onehot = (chosen[..., None] == jnp.arange(count, dtype=jnp.int32)).astype(jnp.int32)
    before = jnp.cumsum(onehot, axis=-2) - onehot
    return jnp.sum(before * onehot, axis=-1)


def attention_kernel(query_ref, key_ref, value_ref, out_ref, *, scale):
    scores = lax.dot_general(
        query_ref[...],
        key_ref[...],
        (((1,), (1,)), ((), ())),
        preferred_element_type=jnp.float32,
    ) * scale
    scores = scores - jnp.max(scores, axis=-1, keepdims=True)
    weights = jnp.exp(scores)
    probs = (weights / jnp.sum(weights, axis=-1, keepdims=True)).astype(jnp.bfloat16)
    out_ref[...] = jnp.dot(probs, value_ref[...], preferred_element_type=jnp.float32).astype(
        out_ref.dtype
    )


def attention(whole, scale, interpret=False):
    _, pairs, seq_len, head_size = whole.shape
    block = min(256, seq_len)
    return pl.pallas_call(
        functools.partial(attention_kernel, scale=scale),
        grid=(pairs, seq_len // block),
        in_specs=[
            pl.BlockSpec((None, None, block, head_size), lambda p, i: (0, p, i, 0)),
            pl.BlockSpec((None, None, seq_len, head_size), lambda p, i: (1, p, 0, 0)),
            pl.BlockSpec((None, None, seq_len, head_size), lambda p, i: (2, p, 0, 0)),
        ],
        out_specs=pl.BlockSpec((None, block, head_size), lambda p, i: (p, i, 0)),
        out_shape=jax.ShapeDtypeStruct((pairs, seq_len, head_size), whole.dtype),
        interpret=interpret,
    )(whole, whole, whole)


def local(
    tokens,
    expert_ids,
    gate_probs,
    norm_gain,
    expert_gate,
    expert_up,
    expert_down,
    teacher_gain,
    teacher_qkv,
    qk_gain,
    teacher_out,
    critic_in,
    critic_out,
):
    seq_dev = tokens.shape[1]
    images = tokens.shape[2]
    width = tokens.shape[3]
    tok_count = seq_dev * images
    n_owner = lax.axis_size("expert")
    n_replica = lax.axis_size("rep")
    exp_local = expert_gate.shape[0]
    expert_total = exp_local * n_owner
    capacity = max(2, tok_count * 10 // (4 * expert_total))
    gate_full = lax.all_gather(expert_gate, "rep", axis=2, tiled=True)
    up_full = lax.all_gather(expert_up, "rep", axis=2, tiled=True)
    down_parts = [
        lax.all_gather(expert_down[j], "rep", axis=0, tiled=True) for j in range(exp_local)
    ]
    qkv_full = lax.all_gather(teacher_qkv, "rep", axis=2, tiled=True)
    qk_gain_full = lax.all_gather(qk_gain, "rep", axis=1, tiled=True)
    out_full = lax.all_gather(teacher_out, "rep", axis=0, tiled=True)
    residual = tokens.reshape(tok_count, width).astype(jnp.float32)
    normed = norm_rows(residual, norm_gain).astype(jnp.bfloat16)
    chosen = expert_ids.reshape(2 * tok_count)
    slot_index = slot_numbers(chosen, expert_total)
    gate_value = gate_probs.reshape(2 * tok_count)
    target = chosen * capacity + slot_index
    rows_all = jnp.arange(expert_total * capacity, dtype=jnp.int32)
    target_pair = target.reshape(tok_count, 2)
    first_rows = (target_pair[:, 0:1] == rows_all[None, :]).astype(jnp.bfloat16)
    second_rows = (target_pair[:, 1:2] == rows_all[None, :]).astype(jnp.bfloat16)
    token_rows = first_rows + second_rows
    outgoing = jnp.einsum(
        "tr,td->rd", token_rows, normed, preferred_element_type=jnp.float32
    ).astype(jnp.bfloat16)
    outgoing = outgoing.reshape(n_owner, exp_local * capacity, width)
    arrived = lax.all_to_all(outgoing, "expert", split_axis=0, concat_axis=0, tiled=True)
    arrived = arrived.reshape(n_owner, exp_local, capacity, width)
    gate_part = jnp.einsum(
        "sjcd,jdf->sjcf", arrived, gate_full, preferred_element_type=jnp.float32
    )
    up_part = jnp.einsum("sjcd,jdf->sjcf", arrived, up_full, preferred_element_type=jnp.float32)
    hidden = (jax.nn.silu(gate_part) * up_part).astype(jnp.bfloat16)
    ff_total = hidden.shape[-1]
    ff_part = ff_total // n_replica
    returned_parts = []
    for j, down_w in enumerate(down_parts):
        produced = jnp.zeros(arrived[:, j].shape, jnp.float32)
        for part in range(n_replica):
            low = part * ff_part
            produced = produced + jnp.einsum(
                "scf,fd->scd",
                hidden[:, j, :, low:low + ff_part],
                down_w[low:low + ff_part],
                preferred_element_type=jnp.float32,
            ).astype(jnp.bfloat16).astype(jnp.float32)
        returned_parts.append(
            lax.all_to_all(
                produced.astype(jnp.bfloat16), "expert", split_axis=0, concat_axis=0, tiled=True
            )
        )
    returned = jnp.stack(returned_parts, axis=1).reshape(expert_total * capacity, width)
    gate_pair = gate_value.reshape(tok_count, 2)
    combined = jnp.dot(first_rows, returned, preferred_element_type=jnp.float32) * gate_pair[
        :, 0:1
    ] + jnp.dot(second_rows, returned, preferred_element_type=jnp.float32) * gate_pair[:, 1:2]
    mixed = (residual + combined).astype(jnp.bfloat16)
    teacher_in = norm_rows(mixed.astype(jnp.float32), teacher_gain).astype(jnp.bfloat16)
    teacher_in = teacher_in.reshape(seq_dev, images, width)
    mixed = mixed.reshape(seq_dev, images, width)
    heads_all = qkv_full.shape[2]
    head_size = qkv_full.shape[3]
    chunks = images if (heads_all % n_owner == 0) else 1
    per_chunk = images // chunks
    features_parts = []
    logits_parts = []
    grouped_parts = []
    for chunk in range(chunks):
        chunk_in = teacher_in[:, chunk * per_chunk:(chunk + 1) * per_chunk]
        if grouped_parts:
            chunk_in, grouped_parts[-1] = lax.optimization_barrier((chunk_in, grouped_parts[-1]))
        grouped_parts.append(project(chunk_in, qkv_full, qk_gain_full))
    for chunk in range(chunks):
        features, logits = teach(
            grouped_parts[chunk], mixed[:, chunk * per_chunk:(chunk + 1) * per_chunk], out_full,
            critic_in, critic_out, n_replica,
        )
        features_parts.append(features)
        logits_parts.append(logits)
    features = jnp.concatenate(features_parts, axis=1)
    logits = jnp.concatenate(logits_parts, axis=1)
    return (features.reshape(1, seq_dev, images, width), logits.reshape(1, seq_dev, images))


def project(teacher_in, qkv_full, qk_gain_full):
    seq_dev, images, width = teacher_in.shape
    heads_all = qkv_full.shape[2]
    head_size = qkv_full.shape[3]
    projected = jnp.einsum(
        "sid,djhe->jihse", teacher_in, qkv_full, preferred_element_type=jnp.float32
    )
    query = norm_rows(projected[0], qk_gain_full[0][:, None, :])
    keyed = norm_rows(projected[1], qk_gain_full[1][:, None, :])
    projected = jnp.stack([query, keyed, projected[2]]).astype(jnp.bfloat16)
    return projected.reshape(3, images * heads_all, seq_dev, head_size)


def teach(grouped, mixed, out_full, critic_in, critic_out, n_replica):
    seq_dev, images, width = mixed.shape
    heads_all = out_full.shape[0]
    head_size = out_full.shape[1]
    whole = lax.all_to_all(grouped, "expert", split_axis=1, concat_axis=2, tiled=True)
    attended = attention(whole, head_size ** (-0.5))
    gathered_heads = lax.all_to_all(attended, "expert", split_axis=1, concat_axis=0, tiled=True)
    gathered_heads = gathered_heads.reshape(images, heads_all, seq_dev, head_size)
    heads_part = heads_all // n_replica
    projected_out = jnp.zeros((seq_dev, images, width), jnp.float32)
    for part in range(n_replica):
        low = part * heads_part
        projected_out = projected_out + jnp.einsum(
            "ihse,hed->sid",
            gathered_heads[:, low:low + heads_part],
            out_full[low:low + heads_part],
            preferred_element_type=jnp.float32,
        ).astype(jnp.bfloat16).astype(jnp.float32)
    features = (mixed.astype(jnp.float32) + projected_out).astype(jnp.bfloat16)
    critic_hidden = jax.nn.gelu(
        jnp.dot(
            features.reshape(seq_dev * images, width), critic_in, preferred_element_type=jnp.float32
        ),
        approximate=True,
    )
    logits = jnp.dot(
        critic_hidden,
        critic_out,
        precision=lax.Precision.HIGHEST,
        preferred_element_type=jnp.float32,
    )
    return features, logits.reshape(seq_dev, images)


def solution(mesh):
    return jax.shard_map(
        local,
        mesh=mesh,
        in_specs=(
            P("rep", "expert", None, None),
            P("rep", "expert", None, None),
            P("rep", "expert", None, None),
            P(),
            P("expert", None, "rep"),
            P("expert", None, "rep"),
            P("expert", "rep", None),
            P(),
            P(None, None, "rep", None),
            P(None, "rep", None),
            P("rep", None, None),
            P(),
            P(),
        ),
        out_specs=(P("rep", "expert", None, None), P("rep", "expert", None)),
        check_vma=False,
    )
```

```python
import functools

import jax
import jax.numpy as jnp
from jax import lax
from jax.experimental import pallas as pl
from jax.sharding import PartitionSpec as P


def norm_rows(values, gain):
    return values * lax.rsqrt(jnp.mean(values * values, axis=-1, keepdims=True) + 1e-06) * gain


def slot_numbers(chosen, count):
    onehot = (chosen[..., None] == jnp.arange(count, dtype=jnp.int32)).astype(jnp.int32)
    before = jnp.cumsum(onehot, axis=-2) - onehot
    return jnp.sum(before * onehot, axis=-1)


def attention_kernel(query_ref, key_ref, value_ref, out_ref, *, scale):
    scores = lax.dot_general(
        query_ref[...],
        key_ref[...],
        (((1,), (1,)), ((), ())),
        preferred_element_type=jnp.float32,
    ) * scale
    scores = scores - jnp.max(scores, axis=-1, keepdims=True)
    weights = jnp.exp(scores)
    probs = (weights / jnp.sum(weights, axis=-1, keepdims=True)).astype(jnp.bfloat16)
    out_ref[...] = jnp.dot(probs, value_ref[...], preferred_element_type=jnp.float32).astype(
        out_ref.dtype
    )


def attention(sent, scale, interpret=False):
    query, key, value = sent
    pairs, seq_len, head_size = query.shape
    block = min(256, seq_len)
    return pl.pallas_call(
        functools.partial(attention_kernel, scale=scale),
        grid=(pairs, seq_len // block),
        in_specs=[
            pl.BlockSpec((None, block, head_size), lambda p, i: (p, i, 0)),
            pl.BlockSpec((None, seq_len, head_size), lambda p, i: (p, 0, 0)),
            pl.BlockSpec((None, seq_len, head_size), lambda p, i: (p, 0, 0)),
        ],
        out_specs=pl.BlockSpec((None, block, head_size), lambda p, i: (p, i, 0)),
        out_shape=jax.ShapeDtypeStruct((pairs, seq_len, head_size), query.dtype),
        interpret=interpret,
    )(query, key, value)


def local(
    tokens,
    expert_ids,
    gate_probs,
    norm_gain,
    expert_gate,
    expert_up,
    expert_down,
    teacher_gain,
    teacher_qkv,
    qk_gain,
    teacher_out,
    critic_in,
    critic_out,
):
    seq_dev = tokens.shape[1]
    images = tokens.shape[2]
    width = tokens.shape[3]
    tok_count = seq_dev * images
    n_owner = lax.axis_size("expert")
    n_replica = lax.axis_size("rep")
    exp_local = expert_gate.shape[0]
    expert_total = exp_local * n_owner
    capacity = max(2, tok_count * 10 // (4 * expert_total))
    gate_full = lax.all_gather(expert_gate, "rep", axis=2, tiled=True)
    up_full = lax.all_gather(expert_up, "rep", axis=2, tiled=True)
    down_parts = [
        lax.all_gather(expert_down[j], "rep", axis=0, tiled=True) for j in range(exp_local)
    ]
    qkv_full = [
        lax.all_gather(teacher_qkv[:, j], "rep", axis=1, tiled=True) for j in range(3)
    ]
    qk_gain_full = lax.all_gather(qk_gain, "rep", axis=1, tiled=True)
    out_full = lax.all_gather(teacher_out, "rep", axis=0, tiled=True)
    residual = tokens.reshape(tok_count, width).astype(jnp.float32)
    normed = norm_rows(residual, norm_gain).astype(jnp.bfloat16)
    chosen = expert_ids.reshape(2 * tok_count)
    slot_index = slot_numbers(chosen, expert_total)
    gate_value = gate_probs.reshape(2 * tok_count)
    target = chosen * capacity + slot_index
    rows_all = jnp.arange(expert_total * capacity, dtype=jnp.int32)
    target_pair = target.reshape(tok_count, 2)
    first_rows = (target_pair[:, 0:1] == rows_all[None, :]).astype(jnp.bfloat16)
    second_rows = (target_pair[:, 1:2] == rows_all[None, :]).astype(jnp.bfloat16)
    token_rows = first_rows + second_rows
    outgoing = jnp.einsum(
        "tr,td->rd", token_rows, normed, preferred_element_type=jnp.float32
    ).astype(jnp.bfloat16)
    outgoing = outgoing.reshape(n_owner, exp_local * capacity, width)
    arrived = lax.all_to_all(outgoing, "expert", split_axis=0, concat_axis=0, tiled=True)
    arrived = arrived.reshape(n_owner, exp_local, capacity, width)
    gate_part = jnp.einsum(
        "sjcd,jdf->sjcf", arrived, gate_full, preferred_element_type=jnp.float32
    )
    up_part = jnp.einsum("sjcd,jdf->sjcf", arrived, up_full, preferred_element_type=jnp.float32)
    hidden = (jax.nn.silu(gate_part) * up_part).astype(jnp.bfloat16)
    ff_total = hidden.shape[-1]
    ff_part = ff_total // n_replica
    returned_parts = []
    for j, down_w in enumerate(down_parts):
        produced = jnp.zeros(arrived[:, j].shape, jnp.float32)
        for part in range(n_replica):
            low = part * ff_part
            produced = produced + jnp.einsum(
                "scf,fd->scd",
                hidden[:, j, :, low:low + ff_part],
                down_w[low:low + ff_part],
                preferred_element_type=jnp.float32,
            ).astype(jnp.bfloat16).astype(jnp.float32)
        returned_parts.append(
            lax.all_to_all(
                produced.astype(jnp.bfloat16), "expert", split_axis=0, concat_axis=0, tiled=True
            )
        )
    returned = jnp.stack(returned_parts, axis=1).reshape(expert_total * capacity, width)
    gate_pair = gate_value.reshape(tok_count, 2)
    combined = jnp.dot(first_rows, returned, preferred_element_type=jnp.float32) * gate_pair[
        :, 0:1
    ] + jnp.dot(second_rows, returned, preferred_element_type=jnp.float32) * gate_pair[:, 1:2]
    mixed = (residual + combined).astype(jnp.bfloat16)
    teacher_in = norm_rows(mixed.astype(jnp.float32), teacher_gain).astype(jnp.bfloat16)
    teacher_in = teacher_in.reshape(seq_dev, images, width)
    mixed = mixed.reshape(seq_dev, images, width)
    heads_all = qkv_full[0].shape[1]
    head_size = qkv_full[0].shape[2]
    chunks = images if (heads_all % n_owner == 0) else 1
    per_chunk = images // chunks
    features_parts = []
    logits_parts = []
    sent_parts = []
    for chunk in range(chunks):
        chunk_in = teacher_in[:, chunk * per_chunk:(chunk + 1) * per_chunk]
        if sent_parts:
            chunk_in, sent_parts[-1] = lax.optimization_barrier((chunk_in, sent_parts[-1]))
        sent = []
        for j in range(3):
            gain = qk_gain_full[j] if j < 2 else None
            sent.append(project(chunk_in, qkv_full[j], gain))
        sent_parts.append(tuple(sent))
    for chunk in range(chunks):
        features, logits = teach(
            sent_parts[chunk], mixed[:, chunk * per_chunk:(chunk + 1) * per_chunk], out_full,
            critic_in, critic_out, n_replica,
        )
        features_parts.append(features)
        logits_parts.append(logits)
    features = jnp.concatenate(features_parts, axis=1)
    logits = jnp.concatenate(logits_parts, axis=1)
    return (features.reshape(1, seq_dev, images, width), logits.reshape(1, seq_dev, images))


def project(teacher_in, weights, gain):
    seq_dev, images, width = teacher_in.shape
    heads_all = weights.shape[1]
    head_size = weights.shape[2]
    projected = jnp.einsum(
        "sid,dhe->ihse", teacher_in, weights, preferred_element_type=jnp.float32
    )
    if gain is not None:
        projected = norm_rows(projected, gain[:, None, :])
    projected = projected.astype(jnp.bfloat16).reshape(images * heads_all, seq_dev, head_size)
    return lax.all_to_all(projected, "expert", split_axis=0, concat_axis=1, tiled=True)


def teach(sent, mixed, out_full, critic_in, critic_out, n_replica):
    seq_dev, images, width = mixed.shape
    heads_all = out_full.shape[0]
    head_size = out_full.shape[1]
    attended = attention(sent, head_size ** (-0.5))
    gathered_heads = lax.all_to_all(attended, "expert", split_axis=1, concat_axis=0, tiled=True)
    gathered_heads = gathered_heads.reshape(images, heads_all, seq_dev, head_size)
    heads_part = heads_all // n_replica
    projected_out = jnp.zeros((seq_dev, images, width), jnp.float32)
    for part in range(n_replica):
        low = part * heads_part
        projected_out = projected_out + jnp.einsum(
            "ihse,hed->sid",
            gathered_heads[:, low:low + heads_part],
            out_full[low:low + heads_part],
            preferred_element_type=jnp.float32,
        ).astype(jnp.bfloat16).astype(jnp.float32)
    features = (mixed.astype(jnp.float32) + projected_out).astype(jnp.bfloat16)
    critic_hidden = jax.nn.gelu(
        jnp.dot(
            features.reshape(seq_dev * images, width), critic_in, preferred_element_type=jnp.float32
        ),
        approximate=True,
    )
    logits = jnp.dot(
        critic_hidden,
        critic_out,
        precision=lax.Precision.HIGHEST,
        preferred_element_type=jnp.float32,
    )
    return features, logits.reshape(seq_dev, images)


def solution(mesh):
    return jax.shard_map(
        local,
        mesh=mesh,
        in_specs=(
            P("rep", "expert", None, None),
            P("rep", "expert", None, None),
            P("rep", "expert", None, None),
            P(),
            P("expert", None, "rep"),
            P("expert", None, "rep"),
            P("expert", "rep", None),
            P(),
            P(None, None, "rep", None),
            P(None, "rep", None),
            P("rep", None, None),
            P(),
            P(),
        ),
        out_specs=(P("rep", "expert", None, None), P("rep", "expert", None)),
        check_vma=False,
    )
```

```python
import functools

import jax
import jax.numpy as jnp
from jax import lax
from jax.experimental import pallas as pl
from jax.sharding import PartitionSpec as P


def norm_rows(values, gain):
    return values * lax.rsqrt(jnp.mean(values * values, axis=-1, keepdims=True) + 1e-06) * gain


def slot_numbers(chosen, count):
    onehot = (chosen[..., None] == jnp.arange(count, dtype=jnp.int32)).astype(jnp.int32)
    before = jnp.cumsum(onehot, axis=-2) - onehot
    return jnp.sum(before * onehot, axis=-1)


def attention_kernel(query_ref, key_ref, value_ref, out_ref, *, scale):
    scores = lax.dot_general(
        query_ref[...],
        key_ref[...],
        (((1,), (1,)), ((), ())),
        preferred_element_type=jnp.float32,
    ) * scale
    scores = scores - jnp.max(scores, axis=-1, keepdims=True)
    weights = jnp.exp(scores)
    probs = (weights / jnp.sum(weights, axis=-1, keepdims=True)).astype(jnp.bfloat16)
    out_ref[...] = jnp.dot(probs, value_ref[...], preferred_element_type=jnp.float32).astype(
        out_ref.dtype
    )


def attention(whole, scale, interpret=False):
    _, pairs, seq_len, head_size = whole.shape
    block = min(512, seq_len)
    return pl.pallas_call(
        functools.partial(attention_kernel, scale=scale),
        grid=(pairs, seq_len // block),
        in_specs=[
            pl.BlockSpec((None, None, block, head_size), lambda p, i: (0, p, i, 0)),
            pl.BlockSpec((None, None, seq_len, head_size), lambda p, i: (1, p, 0, 0)),
            pl.BlockSpec((None, None, seq_len, head_size), lambda p, i: (2, p, 0, 0)),
        ],
        out_specs=pl.BlockSpec((None, block, head_size), lambda p, i: (p, i, 0)),
        out_shape=jax.ShapeDtypeStruct((pairs, seq_len, head_size), whole.dtype),
        interpret=interpret,
    )(whole, whole, whole)


def local(
    tokens,
    expert_ids,
    gate_probs,
    norm_gain,
    expert_gate,
    expert_up,
    expert_down,
    teacher_gain,
    teacher_qkv,
    qk_gain,
    teacher_out,
    critic_in,
    critic_out,
):
    seq_dev = tokens.shape[1]
    images = tokens.shape[2]
    width = tokens.shape[3]
    tok_count = seq_dev * images
    n_owner = lax.axis_size("expert")
    n_replica = lax.axis_size("rep")
    exp_local = expert_gate.shape[0]
    expert_total = exp_local * n_owner
    capacity = max(2, tok_count * 10 // (4 * expert_total))
    gate_full = lax.all_gather(expert_gate, "rep", axis=2, tiled=True)
    up_full = lax.all_gather(expert_up, "rep", axis=2, tiled=True)
    down_parts = [
        lax.all_gather(expert_down[j], "rep", axis=0, tiled=True) for j in range(exp_local)
    ]
    qkv_full = lax.all_gather(teacher_qkv, "rep", axis=2, tiled=True)
    qk_gain_full = lax.all_gather(qk_gain, "rep", axis=1, tiled=True)
    out_full = lax.all_gather(teacher_out, "rep", axis=0, tiled=True)
    residual = tokens.reshape(tok_count, width).astype(jnp.float32)
    normed = norm_rows(residual, norm_gain).astype(jnp.bfloat16)
    chosen = expert_ids.reshape(2 * tok_count)
    slot_index = slot_numbers(chosen, expert_total)
    gate_value = gate_probs.reshape(2 * tok_count)
    target = chosen * capacity + slot_index
    rows_all = jnp.arange(expert_total * capacity, dtype=jnp.int32)
    target_pair = target.reshape(tok_count, 2)
    first_rows = (target_pair[:, 0:1] == rows_all[None, :]).astype(jnp.bfloat16)
    second_rows = (target_pair[:, 1:2] == rows_all[None, :]).astype(jnp.bfloat16)
    token_rows = first_rows + second_rows
    outgoing = jnp.einsum(
        "tr,td->rd", token_rows, normed, preferred_element_type=jnp.float32
    ).astype(jnp.bfloat16)
    outgoing = outgoing.reshape(n_owner, exp_local * capacity, width)
    arrived = lax.all_to_all(outgoing, "expert", split_axis=0, concat_axis=0, tiled=True)
    arrived = arrived.reshape(n_owner, exp_local, capacity, width)
    gate_part = jnp.einsum(
        "sjcd,jdf->sjcf", arrived, gate_full, preferred_element_type=jnp.float32
    )
    up_part = jnp.einsum("sjcd,jdf->sjcf", arrived, up_full, preferred_element_type=jnp.float32)
    hidden = (jax.nn.silu(gate_part) * up_part).astype(jnp.bfloat16)
    ff_total = hidden.shape[-1]
    ff_part = ff_total // n_replica
    returned_parts = []
    for j, down_w in enumerate(down_parts):
        produced = jnp.zeros(arrived[:, j].shape, jnp.float32)
        for part in range(n_replica):
            low = part * ff_part
            produced = produced + jnp.einsum(
                "scf,fd->scd",
                hidden[:, j, :, low:low + ff_part],
                down_w[low:low + ff_part],
                preferred_element_type=jnp.float32,
            ).astype(jnp.bfloat16).astype(jnp.float32)
        returned_parts.append(
            lax.all_to_all(
                produced.astype(jnp.bfloat16), "expert", split_axis=0, concat_axis=0, tiled=True
            )
        )
    returned = jnp.stack(returned_parts, axis=1).reshape(expert_total * capacity, width)
    gate_pair = gate_value.reshape(tok_count, 2)
    combined = jnp.dot(first_rows, returned, preferred_element_type=jnp.float32) * gate_pair[
        :, 0:1
    ] + jnp.dot(second_rows, returned, preferred_element_type=jnp.float32) * gate_pair[:, 1:2]
    mixed = (residual + combined).astype(jnp.bfloat16)
    teacher_in = norm_rows(mixed.astype(jnp.float32), teacher_gain).astype(jnp.bfloat16)
    teacher_in = teacher_in.reshape(seq_dev, images, width)
    mixed = mixed.reshape(seq_dev, images, width)
    heads_all = qkv_full.shape[2]
    head_size = qkv_full.shape[3]
    chunks = images if (heads_all % n_owner == 0) else 1
    per_chunk = images // chunks
    features_parts = []
    logits_parts = []
    grouped_parts = []
    for chunk in range(chunks):
        chunk_in = teacher_in[:, chunk * per_chunk:(chunk + 1) * per_chunk]
        if grouped_parts:
            chunk_in, grouped_parts[-1] = lax.optimization_barrier((chunk_in, grouped_parts[-1]))
        grouped_parts.append(project(chunk_in, qkv_full, qk_gain_full))
    for chunk in range(chunks):
        features, logits = teach(
            grouped_parts[chunk], mixed[:, chunk * per_chunk:(chunk + 1) * per_chunk], out_full,
            critic_in, critic_out, n_replica,
        )
        features_parts.append(features)
        logits_parts.append(logits)
    features = jnp.concatenate(features_parts, axis=1)
    logits = jnp.concatenate(logits_parts, axis=1)
    return (features.reshape(1, seq_dev, images, width), logits.reshape(1, seq_dev, images))


def project(teacher_in, qkv_full, qk_gain_full):
    seq_dev, images, width = teacher_in.shape
    heads_all = qkv_full.shape[2]
    head_size = qkv_full.shape[3]
    projected = jnp.einsum(
        "sid,djhe->jihse", teacher_in, qkv_full, preferred_element_type=jnp.float32
    )
    query = norm_rows(projected[0], qk_gain_full[0][:, None, :])
    keyed = norm_rows(projected[1], qk_gain_full[1][:, None, :])
    projected = jnp.stack([query, keyed, projected[2]]).astype(jnp.bfloat16)
    return projected.reshape(3, images * heads_all, seq_dev, head_size)


def teach(grouped, mixed, out_full, critic_in, critic_out, n_replica):
    seq_dev, images, width = mixed.shape
    heads_all = out_full.shape[0]
    head_size = out_full.shape[1]
    whole = lax.all_to_all(grouped, "expert", split_axis=1, concat_axis=2, tiled=True)
    attended = attention(whole, head_size ** (-0.5))
    gathered_heads = lax.all_to_all(attended, "expert", split_axis=1, concat_axis=0, tiled=True)
    gathered_heads = gathered_heads.reshape(images, heads_all, seq_dev, head_size)
    heads_part = heads_all // n_replica
    projected_out = jnp.zeros((seq_dev, images, width), jnp.float32)
    for part in range(n_replica):
        low = part * heads_part
        projected_out = projected_out + jnp.einsum(
            "ihse,hed->sid",
            gathered_heads[:, low:low + heads_part],
            out_full[low:low + heads_part],
            preferred_element_type=jnp.float32,
        ).astype(jnp.bfloat16).astype(jnp.float32)
    features = (mixed.astype(jnp.float32) + projected_out).astype(jnp.bfloat16)
    critic_hidden = jax.nn.gelu(
        jnp.dot(
            features.reshape(seq_dev * images, width), critic_in, preferred_element_type=jnp.float32
        ),
        approximate=True,
    )
    logits = jnp.dot(
        critic_hidden,
        critic_out,
        precision=lax.Precision.HIGHEST,
        preferred_element_type=jnp.float32,
    )
    return features, logits.reshape(seq_dev, images)


def solution(mesh):
    return jax.shard_map(
        local,
        mesh=mesh,
        in_specs=(
            P("rep", "expert", None, None),
            P("rep", "expert", None, None),
            P("rep", "expert", None, None),
            P(),
            P("expert", None, "rep"),
            P("expert", None, "rep"),
            P("expert", "rep", None),
            P(),
            P(None, None, "rep", None),
            P(None, "rep", None),
            P("rep", None, None),
            P(),
            P(),
        ),
        out_specs=(P("rep", "expert", None, None), P("rep", "expert", None)),
        check_vma=False,
    )
```

```python
import functools

import jax
import jax.numpy as jnp
from jax import lax
from jax.experimental import pallas as pl
from jax.sharding import PartitionSpec as P


def norm_rows(values, gain):
    return values * lax.rsqrt(jnp.mean(values * values, axis=-1, keepdims=True) + 1e-06) * gain


def slot_numbers(chosen, count):
    onehot = (chosen[..., None] == jnp.arange(count, dtype=jnp.int32)).astype(jnp.int32)
    before = jnp.cumsum(onehot, axis=-2) - onehot
    return jnp.sum(before * onehot, axis=-1)


def attention_kernel(query_ref, key_ref, value_ref, out_ref, *, scale):
    scores = lax.dot_general(
        query_ref[...],
        key_ref[...],
        (((1,), (1,)), ((), ())),
        preferred_element_type=jnp.float32,
    ) * scale
    scores = scores - jnp.max(scores, axis=-1, keepdims=True)
    weights = jnp.exp(scores)
    probs = (weights / jnp.sum(weights, axis=-1, keepdims=True)).astype(jnp.bfloat16)
    out_ref[...] = jnp.dot(probs, value_ref[...], preferred_element_type=jnp.float32).astype(
        out_ref.dtype
    )


def attention(whole, scale, interpret=False):
    _, pairs, seq_len, head_size = whole.shape
    block = min(128, seq_len)
    return pl.pallas_call(
        functools.partial(attention_kernel, scale=scale),
        grid=(pairs, seq_len // block),
        in_specs=[
            pl.BlockSpec((None, None, block, head_size), lambda p, i: (0, p, i, 0)),
            pl.BlockSpec((None, None, seq_len, head_size), lambda p, i: (1, p, 0, 0)),
            pl.BlockSpec((None, None, seq_len, head_size), lambda p, i: (2, p, 0, 0)),
        ],
        out_specs=pl.BlockSpec((None, block, head_size), lambda p, i: (p, i, 0)),
        out_shape=jax.ShapeDtypeStruct((pairs, seq_len, head_size), whole.dtype),
        interpret=interpret,
    )(whole, whole, whole)


def local(
    tokens,
    expert_ids,
    gate_probs,
    norm_gain,
    expert_gate,
    expert_up,
    expert_down,
    teacher_gain,
    teacher_qkv,
    qk_gain,
    teacher_out,
    critic_in,
    critic_out,
):
    seq_dev = tokens.shape[1]
    images = tokens.shape[2]
    width = tokens.shape[3]
    tok_count = seq_dev * images
    n_owner = lax.axis_size("expert")
    n_replica = lax.axis_size("rep")
    exp_local = expert_gate.shape[0]
    expert_total = exp_local * n_owner
    capacity = max(2, tok_count * 10 // (4 * expert_total))
    gate_full = lax.all_gather(expert_gate, "rep", axis=2, tiled=True)
    up_full = lax.all_gather(expert_up, "rep", axis=2, tiled=True)
    down_parts = [
        lax.all_gather(expert_down[j], "rep", axis=0, tiled=True) for j in range(exp_local)
    ]
    qkv_full = lax.all_gather(teacher_qkv, "rep", axis=2, tiled=True)
    qk_gain_full = lax.all_gather(qk_gain, "rep", axis=1, tiled=True)
    out_full = lax.all_gather(teacher_out, "rep", axis=0, tiled=True)
    residual = tokens.reshape(tok_count, width).astype(jnp.float32)
    normed = norm_rows(residual, norm_gain).astype(jnp.bfloat16)
    chosen = expert_ids.reshape(2 * tok_count)
    slot_index = slot_numbers(chosen, expert_total)
    gate_value = gate_probs.reshape(2 * tok_count)
    target = chosen * capacity + slot_index
    rows_all = jnp.arange(expert_total * capacity, dtype=jnp.int32)
    target_pair = target.reshape(tok_count, 2)
    first_rows = (target_pair[:, 0:1] == rows_all[None, :]).astype(jnp.bfloat16)
    second_rows = (target_pair[:, 1:2] == rows_all[None, :]).astype(jnp.bfloat16)
    token_rows = first_rows + second_rows
    outgoing = jnp.einsum(
        "tr,td->rd", token_rows, normed, preferred_element_type=jnp.float32
    ).astype(jnp.bfloat16)
    outgoing = outgoing.reshape(n_owner, exp_local * capacity, width)
    arrived = lax.all_to_all(outgoing, "expert", split_axis=0, concat_axis=0, tiled=True)
    arrived = arrived.reshape(n_owner, exp_local, capacity, width)
    gate_part = jnp.einsum(
        "sjcd,jdf->sjcf", arrived, gate_full, preferred_element_type=jnp.float32
    )
    up_part = jnp.einsum("sjcd,jdf->sjcf", arrived, up_full, preferred_element_type=jnp.float32)
    hidden = (jax.nn.silu(gate_part) * up_part).astype(jnp.bfloat16)
    ff_total = hidden.shape[-1]
    ff_part = ff_total // n_replica
    returned_parts = []
    for j, down_w in enumerate(down_parts):
        produced = jnp.zeros(arrived[:, j].shape, jnp.float32)
        for part in range(n_replica):
            low = part * ff_part
            produced = produced + jnp.einsum(
                "scf,fd->scd",
                hidden[:, j, :, low:low + ff_part],
                down_w[low:low + ff_part],
                preferred_element_type=jnp.float32,
            ).astype(jnp.bfloat16).astype(jnp.float32)
        returned_parts.append(
            lax.all_to_all(
                produced.astype(jnp.bfloat16), "expert", split_axis=0, concat_axis=0, tiled=True
            )
        )
    returned = jnp.stack(returned_parts, axis=1).reshape(expert_total * capacity, width)
    gate_pair = gate_value.reshape(tok_count, 2)
    combined = jnp.dot(first_rows, returned, preferred_element_type=jnp.float32) * gate_pair[
        :, 0:1
    ] + jnp.dot(second_rows, returned, preferred_element_type=jnp.float32) * gate_pair[:, 1:2]
    mixed = (residual + combined).astype(jnp.bfloat16)
    teacher_in = norm_rows(mixed.astype(jnp.float32), teacher_gain).astype(jnp.bfloat16)
    teacher_in = teacher_in.reshape(seq_dev, images, width)
    mixed = mixed.reshape(seq_dev, images, width)
    heads_all = qkv_full.shape[2]
    head_size = qkv_full.shape[3]
    chunks = images if (heads_all % n_owner == 0) else 1
    per_chunk = images // chunks
    features_parts = []
    logits_parts = []
    grouped_parts = []
    for chunk in range(chunks):
        chunk_in = teacher_in[:, chunk * per_chunk:(chunk + 1) * per_chunk]
        if grouped_parts:
            chunk_in, grouped_parts[-1] = lax.optimization_barrier((chunk_in, grouped_parts[-1]))
        grouped_parts.append(project(chunk_in, qkv_full, qk_gain_full))
    for chunk in range(chunks):
        features, logits = teach(
            grouped_parts[chunk], mixed[:, chunk * per_chunk:(chunk + 1) * per_chunk], out_full,
            critic_in, critic_out, n_replica,
        )
        features_parts.append(features)
        logits_parts.append(logits)
    features = jnp.concatenate(features_parts, axis=1)
    logits = jnp.concatenate(logits_parts, axis=1)
    return (features.reshape(1, seq_dev, images, width), logits.reshape(1, seq_dev, images))


def project(teacher_in, qkv_full, qk_gain_full):
    seq_dev, images, width = teacher_in.shape
    heads_all = qkv_full.shape[2]
    head_size = qkv_full.shape[3]
    projected = jnp.einsum(
        "sid,djhe->jihse", teacher_in, qkv_full, preferred_element_type=jnp.float32
    )
    query = norm_rows(projected[0], qk_gain_full[0][:, None, :])
    keyed = norm_rows(projected[1], qk_gain_full[1][:, None, :])
    projected = jnp.stack([query, keyed, projected[2]]).astype(jnp.bfloat16)
    return projected.reshape(3, images * heads_all, seq_dev, head_size)


def teach(grouped, mixed, out_full, critic_in, critic_out, n_replica):
    seq_dev, images, width = mixed.shape
    heads_all = out_full.shape[0]
    head_size = out_full.shape[1]
    whole = lax.all_to_all(grouped, "expert", split_axis=1, concat_axis=2, tiled=True)
    attended = attention(whole, head_size ** (-0.5))
    gathered_heads = lax.all_to_all(attended, "expert", split_axis=1, concat_axis=0, tiled=True)
    gathered_heads = gathered_heads.reshape(images, heads_all, seq_dev, head_size)
    heads_part = heads_all // n_replica
    projected_out = jnp.zeros((seq_dev, images, width), jnp.float32)
    for part in range(n_replica):
        low = part * heads_part
        projected_out = projected_out + jnp.einsum(
            "ihse,hed->sid",
            gathered_heads[:, low:low + heads_part],
            out_full[low:low + heads_part],
            preferred_element_type=jnp.float32,
        ).astype(jnp.bfloat16).astype(jnp.float32)
    features = (mixed.astype(jnp.float32) + projected_out).astype(jnp.bfloat16)
    critic_hidden = jax.nn.gelu(
        jnp.dot(
            features.reshape(seq_dev * images, width), critic_in, preferred_element_type=jnp.float32
        ),
        approximate=True,
    )
    logits = jnp.dot(
        critic_hidden,
        critic_out,
        precision=lax.Precision.HIGHEST,
        preferred_element_type=jnp.float32,
    )
    return features, logits.reshape(seq_dev, images)


def solution(mesh):
    return jax.shard_map(
        local,
        mesh=mesh,
        in_specs=(
            P("rep", "expert", None, None),
            P("rep", "expert", None, None),
            P("rep", "expert", None, None),
            P(),
            P("expert", None, "rep"),
            P("expert", None, "rep"),
            P("expert", "rep", None),
            P(),
            P(None, None, "rep", None),
            P(None, "rep", None),
            P("rep", None, None),
            P(),
            P(),
        ),
        out_specs=(P("rep", "expert", None, None), P("rep", "expert", None)),
        check_vma=False,
    )
```

```python
import functools

import jax
import jax.numpy as jnp
from jax import lax
from jax.experimental import pallas as pl
from jax.sharding import PartitionSpec as P


def norm_rows(values, gain):
    return values * lax.rsqrt(jnp.mean(values * values, axis=-1, keepdims=True) + 1e-06) * gain


def slot_numbers(chosen, count):
    onehot = (chosen[..., None] == jnp.arange(count, dtype=jnp.int32)).astype(jnp.int32)
    before = jnp.cumsum(onehot, axis=-2) - onehot
    return jnp.sum(before * onehot, axis=-1)


def attention_kernel(query_ref, key_ref, value_ref, out_ref, *, scale):
    scores = lax.dot_general(
        query_ref[...],
        key_ref[...],
        (((1,), (1,)), ((), ())),
        preferred_element_type=jnp.float32,
    ) * scale
    scores = scores - jnp.max(scores, axis=-1, keepdims=True)
    weights = jnp.exp(scores)
    inverse = 1.0 / jnp.sum(weights, axis=-1, keepdims=True)
    probs = (weights * inverse).astype(jnp.bfloat16)
    out_ref[...] = jnp.dot(probs, value_ref[...], preferred_element_type=jnp.float32).astype(
        out_ref.dtype
    )


def attention(whole, scale, interpret=False):
    _, pairs, seq_len, head_size = whole.shape
    block = min(256, seq_len)
    return pl.pallas_call(
        functools.partial(attention_kernel, scale=scale),
        grid=(pairs, seq_len // block),
        in_specs=[
            pl.BlockSpec((None, None, block, head_size), lambda p, i: (0, p, i, 0)),
            pl.BlockSpec((None, None, seq_len, head_size), lambda p, i: (1, p, 0, 0)),
            pl.BlockSpec((None, None, seq_len, head_size), lambda p, i: (2, p, 0, 0)),
        ],
        out_specs=pl.BlockSpec((None, block, head_size), lambda p, i: (p, i, 0)),
        out_shape=jax.ShapeDtypeStruct((pairs, seq_len, head_size), whole.dtype),
        interpret=interpret,
    )(whole, whole, whole)


def local(
    tokens,
    expert_ids,
    gate_probs,
    norm_gain,
    expert_gate,
    expert_up,
    expert_down,
    teacher_gain,
    teacher_qkv,
    qk_gain,
    teacher_out,
    critic_in,
    critic_out,
):
    seq_dev = tokens.shape[1]
    images = tokens.shape[2]
    width = tokens.shape[3]
    tok_count = seq_dev * images
    n_owner = lax.axis_size("expert")
    n_replica = lax.axis_size("rep")
    exp_local = expert_gate.shape[0]
    expert_total = exp_local * n_owner
    capacity = max(2, tok_count * 10 // (4 * expert_total))
    gate_full = lax.all_gather(expert_gate, "rep", axis=2, tiled=True)
    up_full = lax.all_gather(expert_up, "rep", axis=2, tiled=True)
    down_parts = [
        lax.all_gather(expert_down[j], "rep", axis=0, tiled=True) for j in range(exp_local)
    ]
    qkv_full = lax.all_gather(teacher_qkv, "rep", axis=2, tiled=True)
    qk_gain_full = lax.all_gather(qk_gain, "rep", axis=1, tiled=True)
    out_full = lax.all_gather(teacher_out, "rep", axis=0, tiled=True)
    residual = tokens.reshape(tok_count, width).astype(jnp.float32)
    normed = norm_rows(residual, norm_gain).astype(jnp.bfloat16)
    chosen = expert_ids.reshape(2 * tok_count)
    slot_index = slot_numbers(chosen, expert_total)
    gate_value = gate_probs.reshape(2 * tok_count)
    target = chosen * capacity + slot_index
    rows_all = jnp.arange(expert_total * capacity, dtype=jnp.int32)
    target_pair = target.reshape(tok_count, 2)
    first_rows = (target_pair[:, 0:1] == rows_all[None, :]).astype(jnp.bfloat16)
    second_rows = (target_pair[:, 1:2] == rows_all[None, :]).astype(jnp.bfloat16)
    token_rows = first_rows + second_rows
    outgoing = jnp.einsum(
        "tr,td->rd", token_rows, normed, preferred_element_type=jnp.float32
    ).astype(jnp.bfloat16)
    outgoing = outgoing.reshape(n_owner, exp_local * capacity, width)
    arrived = lax.all_to_all(outgoing, "expert", split_axis=0, concat_axis=0, tiled=True)
    arrived = arrived.reshape(n_owner, exp_local, capacity, width)
    gate_part = jnp.einsum(
        "sjcd,jdf->sjcf", arrived, gate_full, preferred_element_type=jnp.float32
    )
    up_part = jnp.einsum("sjcd,jdf->sjcf", arrived, up_full, preferred_element_type=jnp.float32)
    hidden = (jax.nn.silu(gate_part) * up_part).astype(jnp.bfloat16)
    ff_total = hidden.shape[-1]
    ff_part = ff_total // n_replica
    returned_parts = []
    for j, down_w in enumerate(down_parts):
        produced = jnp.zeros(arrived[:, j].shape, jnp.float32)
        for part in range(n_replica):
            low = part * ff_part
            produced = produced + jnp.einsum(
                "scf,fd->scd",
                hidden[:, j, :, low:low + ff_part],
                down_w[low:low + ff_part],
                preferred_element_type=jnp.float32,
            ).astype(jnp.bfloat16).astype(jnp.float32)
        returned_parts.append(
            lax.all_to_all(
                produced.astype(jnp.bfloat16), "expert", split_axis=0, concat_axis=0, tiled=True
            )
        )
    returned = jnp.stack(returned_parts, axis=1).reshape(expert_total * capacity, width)
    gate_pair = gate_value.reshape(tok_count, 2)
    combined = jnp.dot(first_rows, returned, preferred_element_type=jnp.float32) * gate_pair[
        :, 0:1
    ] + jnp.dot(second_rows, returned, preferred_element_type=jnp.float32) * gate_pair[:, 1:2]
    mixed = (residual + combined).astype(jnp.bfloat16)
    teacher_in = norm_rows(mixed.astype(jnp.float32), teacher_gain).astype(jnp.bfloat16)
    teacher_in = teacher_in.reshape(seq_dev, images, width)
    mixed = mixed.reshape(seq_dev, images, width)
    heads_all = qkv_full.shape[2]
    head_size = qkv_full.shape[3]
    chunks = images if (heads_all % n_owner == 0) else 1
    per_chunk = images // chunks
    features_parts = []
    logits_parts = []
    grouped_parts = []
    for chunk in range(chunks):
        chunk_in = teacher_in[:, chunk * per_chunk:(chunk + 1) * per_chunk]
        if grouped_parts:
            chunk_in, grouped_parts[-1] = lax.optimization_barrier((chunk_in, grouped_parts[-1]))
        grouped_parts.append(project(chunk_in, qkv_full, qk_gain_full))
    for chunk in range(chunks):
        features, logits = teach(
            grouped_parts[chunk], mixed[:, chunk * per_chunk:(chunk + 1) * per_chunk], out_full,
            critic_in, critic_out, n_replica,
        )
        features_parts.append(features)
        logits_parts.append(logits)
    features = jnp.concatenate(features_parts, axis=1)
    logits = jnp.concatenate(logits_parts, axis=1)
    return (features.reshape(1, seq_dev, images, width), logits.reshape(1, seq_dev, images))


def project(teacher_in, qkv_full, qk_gain_full):
    seq_dev, images, width = teacher_in.shape
    heads_all = qkv_full.shape[2]
    head_size = qkv_full.shape[3]
    projected = jnp.einsum(
        "sid,djhe->jihse", teacher_in, qkv_full, preferred_element_type=jnp.float32
    )
    query = norm_rows(projected[0], qk_gain_full[0][:, None, :])
    keyed = norm_rows(projected[1], qk_gain_full[1][:, None, :])
    projected = jnp.stack([query, keyed, projected[2]]).astype(jnp.bfloat16)
    return projected.reshape(3, images * heads_all, seq_dev, head_size)


def teach(grouped, mixed, out_full, critic_in, critic_out, n_replica):
    seq_dev, images, width = mixed.shape
    heads_all = out_full.shape[0]
    head_size = out_full.shape[1]
    whole = lax.all_to_all(grouped, "expert", split_axis=1, concat_axis=2, tiled=True)
    attended = attention(whole, head_size ** (-0.5))
    gathered_heads = lax.all_to_all(attended, "expert", split_axis=1, concat_axis=0, tiled=True)
    gathered_heads = gathered_heads.reshape(images, heads_all, seq_dev, head_size)
    heads_part = heads_all // n_replica
    projected_out = jnp.zeros((seq_dev, images, width), jnp.float32)
    for part in range(n_replica):
        low = part * heads_part
        projected_out = projected_out + jnp.einsum(
            "ihse,hed->sid",
            gathered_heads[:, low:low + heads_part],
            out_full[low:low + heads_part],
            preferred_element_type=jnp.float32,
        ).astype(jnp.bfloat16).astype(jnp.float32)
    features = (mixed.astype(jnp.float32) + projected_out).astype(jnp.bfloat16)
    critic_hidden = jax.nn.gelu(
        jnp.dot(
            features.reshape(seq_dev * images, width), critic_in, preferred_element_type=jnp.float32
        ),
        approximate=True,
    )
    logits = jnp.dot(
        critic_hidden,
        critic_out,
        precision=lax.Precision.HIGHEST,
        preferred_element_type=jnp.float32,
    )
    return features, logits.reshape(seq_dev, images)


def solution(mesh):
    return jax.shard_map(
        local,
        mesh=mesh,
        in_specs=(
            P("rep", "expert", None, None),
            P("rep", "expert", None, None),
            P("rep", "expert", None, None),
            P(),
            P("expert", None, "rep"),
            P("expert", None, "rep"),
            P("expert", "rep", None),
            P(),
            P(None, None, "rep", None),
            P(None, "rep", None),
            P("rep", None, None),
            P(),
            P(),
        ),
        out_specs=(P("rep", "expert", None, None), P("rep", "expert", None)),
        check_vma=False,
    )
```
